512 devices in a mesh: tile: 16 (over x_hi, z), eval: 32 (over x_lo, y, core).
Axes of the slice: x: 4 (x_hi: 2, x_lo: 2; x = x_hi * 2 + x_lo), y: 8, z: 8, core: 2. Of those that a mesh axis runs over, the one named last changes fastest.
Arguments:
- target_geom: float32 [6, 128, 4096], P(None, 'tile', 'eval'), may hold values from -1 to 1
- eta: float32 [128, 4096], P('tile', 'eval'), may hold values from -3 to 3
- phi: float32 [128, 4096], P('tile', 'eval'), may hold values from -3 to 3
- sources: float32 [16, 4, 4, 1024], P('tile', None, None, 'eval')
- group_len: int32 [4, 32], replicated, may hold values from 1 to 32, 640 in all within a row
- owner: int32 [16], replicated, may hold values from 0 to 15, each once
Outputs:
- eta_next: float32 [128, 4096], P('tile', 'eval')
- phi_next: float32 [128, 4096], P('tile', 'eval')
- normal_velocity: float32 [128, 4096], P('tile', 'eval')
The draws below stay inside these ranges and needn't reach their ends.
Inputs may be any that keep to these rules, and one draw needn't show every extreme that they name: owner holds distinct tile rows; round r's group is held by tile row owner[r]. `group_len`: each round has some column with all 32 slots live.
All inputs are finite; a program needn't handle non-finite values.
Results may differ from the reference program's by a relative error of at most 0.0001.
Values sent between devices are 32-bit elements; how exact they have to be, the bound alone decides.
No kernel may reach another device: no remote copies, remote signals or barrier semaphores. Data moves between devices by JAX's collectives and lax.ppermute only.
A program may use at most 64 MiB of HBM per device.

```python
import math
import jax
import jax.numpy as jnp
import numpy as np
from jax import lax

SC = 32
ROUNDS = 4
NX = 128
NY = 4096
SRC_COLS = 1024
OWNER_ROWS = 16
N_EVAL = 32


def draw_sources(key, part):
    key_pos = jax.random.fold_in(key, 11)
    key_str = jax.random.fold_in(key, 23)
    shape_pos = (OWNER_ROWS, ROUNDS, 3, SRC_COLS)
    shape_str = (OWNER_ROWS, ROUNDS, 1, SRC_COLS)
    factor = (3.0 / (ROUNDS * SRC_COLS)) ** 0.5
    coords = jax.random.uniform(key_pos, shape_pos, jnp.float32, -1.0, 1.0)
    strength = jax.random.uniform(key_str, shape_str, jnp.float32, -1.0, 1.0) * factor
    return jnp.concatenate([coords, strength], axis=2).astype(jnp.float32)


def shard_levels(stream_key, extent, shards, least, top_value):
    def one(axis_at, shards_of):
        steps = jax.random.uniform(jax.random.fold_in(jax.random.fold_in(stream_key, 6), axis_at), (shards_of,), jnp.float32, least / len(shards), top_value / len(shards))
        return jnp.repeat(jnp.exp(steps), extent[axis_at] // shards_of).reshape((-1,) + (1,) * (len(extent) - axis_at - 1))

    level = one(*shards[0])
    for cut in shards[1:]:
        level = level * one(*cut)
    return level


def profile(count, total, most, skew):
    loads = [(1 << 20) // math.isqrt(rank ** skew) + 1 for rank in range(2, count + 1)]
    rest, given = total - most - (count - 1), [1] * (count - 1)
    while rest > 0:
        free = [i for i in range(count - 1) if given[i] < most]
        mass, left = sum([loads[i] for i in free]), rest
        for i in free:
            addition = min(most - given[i], max(1, left * loads[i] // mass), rest)
            given[i] = given[i] + addition
            rest = rest - addition
    return np.array([most] + given)


def uneven(key, number_of, total, limit, skew):
    if number_of == 2:
        one = jax.random.randint(key, (), max(1, total - limit), min(limit, total - 1) + 1)
        return jnp.stack([one, total - one])
    sizes = jnp.asarray(profile(number_of, total, limit, skew), jnp.int32)
    couples = (number_of - 1) // 2
    source_of, taker = sizes[1:1 + 2 * couples:2], sizes[2:2 + 2 * couples:2]
    margin = jnp.minimum(source_of - 1, limit - taker)
    shifted = jax.random.randint(jax.random.fold_in(key, 1), (couples,), 0, 1 << 20) % (margin + 1)
    sizes = sizes.at[1:1 + 2 * couples:2].set(source_of - shifted).at[2:2 + 2 * couples:2].set(taker + shifted)
    return sizes[jax.random.permutation(jax.random.fold_in(key, 2), number_of)]


def centred(key, extent, scale, reach, pieces=(), kind=jnp.bfloat16):
    array = scale * jax.random.normal(key, extent, jnp.float32)
    if pieces:
        array = array * shard_levels(key, extent, pieces, -0.22, 0.18)
    return jnp.clip(array, -reach, reach).astype(kind)


def setup_inputs(seed: int = 0) -> dict:
    seeds = jax.random.split(jax.random.key(seed), 7)
    return {
        "target_geom": jnp.clip(jax.random.uniform(seeds[0], (6, NX, NY), jnp.float32, -1.0, 1.0) * shard_levels(seeds[0], (6, NX, NY), ((1, 16), (2, 32)), -0.4, 0.0), -1.0, 1.0),
        "eta": centred(seeds[1], (NX, NY), 0.5, 3.0, ((0, 16), (1, 32)), jnp.float32),
        "phi": centred(seeds[2], (NX, NY), 0.5, 3.0, ((0, 16), (1, 32)), jnp.float32),
        "sources": draw_sources(jax.random.fold_in(seeds[6], 71), 0),
        "group_len": jax.vmap(lambda own: uneven(own, N_EVAL, N_EVAL * SC * 5 // 8, SC, 2))(jax.random.split(seeds[4], ROUNDS)).reshape((ROUNDS, N_EVAL)).astype(jnp.int32),
        "owner": jax.random.permutation(seeds[5], OWNER_ROWS).astype(jnp.int32),
    }


EPS2 = 0.05

def kernel_sum(targ, src):
    dx = targ[0][None] - src[0][:, None, None]
    dy = targ[1][None] - src[1][:, None, None]
    dz = targ[2][None] - src[2][:, None, None]
    dist2 = dx * dx + dy * dy + dz * dz + EPS2
    numer = targ[3][None] * dx + targ[4][None] * dy + targ[5][None] * dz
    return lax.optimization_barrier(jnp.sum(src[3][:, None, None] * numer / (dist2 * jnp.sqrt(dist2)), axis=0))

def tendency(ext):
    centre = ext[:, 1:-1, 1:-1]
    grad_x = (ext[:, 2:, 1:-1] - ext[:, :-2, 1:-1]) * 0.5
    grad_y = (ext[:, 1:-1, 2:] - ext[:, 1:-1, :-2]) * 0.5
    slope = 1.0 + grad_x[0] * grad_x[0] + grad_y[0] * grad_y[0]
    velocity = centre[2]
    eta_rate = velocity * slope - (grad_x[1] * grad_x[0] + grad_y[1] * grad_y[0])
    phi_rate = -centre[0] - 0.5 * (grad_x[1] * grad_x[1] + grad_y[1] * grad_y[1]) + 0.5 * velocity * velocity * slope
    return jnp.stack([eta_rate, phi_rate])

def smooth(rim):
    centre = rim[:, 1:-1, 1:-1]
    return (4.0 * centre + rim[:, 2:, 1:-1] + rim[:, :-2, 1:-1] + rim[:, 1:-1, 2:] + rim[:, 1:-1, :-2]) / 8.0

def reference(target_geom, eta, phi, sources, group_len, owner):
    slot_ids = jnp.arange(SRC_COLS, dtype=jnp.int32)
    columns = slot_ids // SC
    within = slot_ids % SC
    blocks = []
    for step in range(ROUNDS):
        block = sources[owner[step], step]
        live = (within < group_len[step][columns]).astype(jnp.float32)
        blocks.append(jnp.concatenate([block[:3], block[3:] * live[None]], axis=0))

    def row_velocity(row):
        total = jnp.zeros((1, NY), jnp.float32)
        for block in blocks:
            total = total + kernel_sum(row[:, None, :], block)
        return total[0]
    rows = jnp.moveaxis(target_geom, 1, 0)
    velocity = lax.map(row_velocity, rows)
    fields = jnp.stack([eta, phi, velocity])
    ext = jnp.pad(fields, ((0, 0), (1, 1), (1, 1)))
    rates = tendency(ext)
    rim = jnp.pad(rates, ((0, 0), (1, 1), (1, 1)))
    smoothed = smooth(rim)
    return (eta + 0.5 * smoothed[0], phi + 0.5 * smoothed[1], velocity)
```

```python
import jax
import jax.numpy as jnp
from jax import lax
from jax.sharding import PartitionSpec as P

ROUNDS = 4


EPS2 = 0.05


def shifted(x, axis, dim, width):
    peers, length = (lax.axis_size(axis), x.shape[dim])
    up = [(i, i + 1) for i in range(peers - 1)]
    down = [(j, i) for i, j in up]
    last = lax.slice_in_dim(x, length - width, length, axis=dim)
    first = lax.slice_in_dim(x, 0, width, axis=dim)
    return lax.ppermute(last, axis, up), lax.ppermute(first, axis, down)


def with_halo(x, sides, width):
    for axis, dim in sides:
        before, after = shifted(x, axis, dim, width)
        x = jnp.concatenate([before, x, after], axis=dim)
    return x


def kernel_sum(targ, src):
    dx = targ[0][None] - src[0][:, None, None]
    dy = targ[1][None] - src[1][:, None, None]
    dz = targ[2][None] - src[2][:, None, None]
    dist2 = dx * dx + dy * dy + dz * dz + EPS2
    numer = targ[3][None] * dx + targ[4][None] * dy + targ[5][None] * dz
    return jnp.sum(src[3][:, None, None] * numer / (dist2 * jnp.sqrt(dist2)), axis=0)


def gather_sources(sources, group_len, owner):
    row = lax.axis_index("tile")
    column = lax.axis_index("eval")
    width = sources.shape[-1]
    live = (jnp.arange(width, dtype=jnp.int32)[None, :] < group_len[:ROUNDS, column][:, None])
    mine = (owner[:ROUNDS] == row)
    local = sources[0]
    scale = jnp.concatenate(
        [jnp.broadcast_to(mine[:, None, None], (ROUNDS, 3, width)),
         (mine[:, None] & live)[:, None, :]], axis=1)
    picked = jnp.where(scale, local, 0.0)
    picked = lax.psum(picked, "tile")
    return lax.all_gather(picked, "eval", axis=2, tiled=True)


def tendency(ext, vel):
    centre = ext[:, 1:-1, 1:-1]
    grad_x = (ext[:, 2:, 1:-1] - ext[:, :-2, 1:-1]) * 0.5
    grad_y = (ext[:, 1:-1, 2:] - ext[:, 1:-1, :-2]) * 0.5
    slope = 1.0 + grad_x[0] * grad_x[0] + grad_y[0] * grad_y[0]
    eta_rate = vel * slope - (grad_x[1] * grad_x[0] + grad_y[1] * grad_y[0])
    phi_rate = (
        -centre[0]
        - 0.5 * (grad_x[1] * grad_x[1] + grad_y[1] * grad_y[1])
        + 0.5 * vel * vel * slope
    )
    return jnp.stack([eta_rate, phi_rate])


def smooth(rim):
    centre = rim[:, 1:-1, 1:-1]
    return (
        4.0 * centre + rim[:, 2:, 1:-1] + rim[:, :-2, 1:-1] + rim[:, 1:-1, 2:] + rim[:, 1:-1, :-2]
    ) / 8.0


def body(target_geom, eta, phi, sources, group_len, owner):
    rows_here, cols_here = eta.shape
    ext = with_halo(jnp.stack([eta, phi]), (("tile", 1), ("eval", 2)), 2)
    stacked = gather_sources(sources, group_len, owner)
    velocity = kernel_sum(target_geom, stacked[0])
    for step in range(1, ROUNDS):
        velocity = velocity + kernel_sum(target_geom, stacked[step])
    up, down = shifted(velocity, "tile", 0, 1)
    left, right = shifted(velocity, "eval", 1, 1)
    vel_rows = jnp.concatenate([up, velocity, down], axis=0)
    side = jnp.zeros((1, 1), jnp.float32)
    vel_left = jnp.concatenate([side, left, side], axis=0)
    vel_right = jnp.concatenate([side, right, side], axis=0)
    vel = jnp.concatenate([vel_left, vel_rows, vel_right], axis=1)
    rates = tendency(ext, vel)
    column = lax.axis_index("eval")
    row_ids = lax.axis_index("tile") * rows_here + jnp.arange(rows_here + 2, dtype=jnp.int32) - 1
    col_ids = column * cols_here + jnp.arange(cols_here + 2, dtype=jnp.int32) - 1
    row_ok = (row_ids >= 0) & (row_ids < rows_here * lax.axis_size("tile"))
    col_ok = (col_ids >= 0) & (col_ids < cols_here * lax.axis_size("eval"))
    inside = (row_ok[:, None] & col_ok[None, :]).astype(jnp.float32)
    smoothed = smooth(rates * inside[None])
    return (eta + 0.5 * smoothed[0], phi + 0.5 * smoothed[1], velocity)


def solution(mesh):
    return jax.shard_map(
        body,
        mesh=mesh,
        in_specs=(
            P(None, "tile", "eval"),
            P("tile", "eval"),
            P("tile", "eval"),
            P("tile", None, None, "eval"),
            P(),
            P(),
        ),
        out_specs=(P("tile", "eval"), P("tile", "eval"), P("tile", "eval")),
        check_vma=False,
    )
```

```python
import functools

import jax
import jax.numpy as jnp
from jax import lax
from jax.experimental import pallas as pl
from jax.experimental.pallas import tpu as pltpu
from jax.sharding import PartitionSpec as P

ROUNDS = 4
SC = 32
CHUNK = 8

EPS2 = 0.05


def copy_for_each(x, axis):
    peers = lax.axis_size(axis)
    return lax.all_to_all(jnp.broadcast_to(x[None], (peers, *x.shape)), axis, 0, 0, tiled=True)


def from_peer(received, me, offset, peers):
    peer = me + offset
    ok = (peer >= 0) & (peer < peers)
    chunk = lax.dynamic_index_in_dim(received, jnp.clip(peer, 0, peers - 1), 0, keepdims=False)
    return jnp.where(ok, chunk, jnp.zeros_like(chunk))


def velocity_kernel(len_ref, src_ref, targ_ref, out_ref):
    tx, ty, tz = targ_ref[0], targ_ref[1], targ_ref[2]
    nx, ny, nz = targ_ref[3], targ_ref[4], targ_ref[5]

    def term(row, slot, acc):
        sx = src_ref[row, slot]
        sy = src_ref[row + 1, slot]
        sz = src_ref[row + 2, slot]
        q = src_ref[row + 3, slot]
        dx = tx - sx
        dy = ty - sy
        dz = tz - sz
        dist2 = dx * dx + dy * dy + dz * dz + EPS2
        numer = nx * dx + ny * dy + nz * dz
        r = lax.rsqrt(dist2)
        return acc + (q * numer) * (r * r * r)

    acc = jnp.zeros(out_ref.shape, jnp.float32)
    for step in range(ROUNDS):
        row = step * 4

        def column(c, acc, step=step, row=row):
            chunks = (len_ref[step, c] + (CHUNK - 1)) // CHUNK

            def chunk(j, acc):
                base = c * SC + j * CHUNK
                for u in range(CHUNK):
                    acc = term(row, base + u, acc)
                return acc

            return lax.fori_loop(0, chunks, chunk, acc)

        acc = lax.fori_loop(0, len_ref.shape[1], column, acc)
    out_ref[...] = acc


def velocity(group_len, src, targ):
    return pl.pallas_call(
        velocity_kernel,
        out_shape=jax.ShapeDtypeStruct(targ.shape[1:], jnp.float32),
        in_specs=[
            pl.BlockSpec(memory_space=pltpu.SMEM),
            pl.BlockSpec(memory_space=pltpu.SMEM),
            pl.BlockSpec(memory_space=pltpu.VMEM),
        ],
        out_specs=pl.BlockSpec(memory_space=pltpu.VMEM),
    )(group_len, src, targ)


def tendency(ext, vel):
    centre = ext[:, 1:-1, 1:-1]
    grad_x = (ext[:, 2:, 1:-1] - ext[:, :-2, 1:-1]) * 0.5
    grad_y = (ext[:, 1:-1, 2:] - ext[:, 1:-1, :-2]) * 0.5
    slope = 1.0 + grad_x[0] * grad_x[0] + grad_y[0] * grad_y[0]
    eta_rate = vel * slope - (grad_x[1] * grad_x[0] + grad_y[1] * grad_y[0])
    phi_rate = (
        -centre[0]
        - 0.5 * (grad_x[1] * grad_x[1] + grad_y[1] * grad_y[1])
        + 0.5 * vel * vel * slope
    )
    return jnp.stack([eta_rate, phi_rate])


def smooth(rim):
    centre = rim[:, 1:-1, 1:-1]
    return (
        4.0 * centre + rim[:, 2:, 1:-1] + rim[:, :-2, 1:-1] + rim[:, 1:-1, 2:] + rim[:, 1:-1, :-2]
    ) / 8.0


def body(target_geom, eta, phi, sources, group_len, owner):
    rows_here, cols_here = eta.shape
    n_tile, n_eval = lax.axis_size("tile"), lax.axis_size("eval")
    row = lax.axis_index("tile")
    column = lax.axis_index("eval")
    width = sources.shape[-1]
    group_len = group_len[:ROUNDS]
    owner = owner[:ROUNDS]

    live = jnp.arange(width, dtype=jnp.int32)[None, :] < group_len[:, column][:, None]
    mine = owner == row
    keep = jnp.concatenate(
        [jnp.broadcast_to(mine[:, None, None], (ROUNDS, 3, width)), (mine[:, None] & live)[:, None, :]],
        axis=1)
    picked = jnp.where(keep, sources[0], 0.0)

    fields = jnp.stack([eta, phi])
    n_src = ROUNDS * 4 * width
    payload = jnp.concatenate([
        picked.reshape(-1),
        fields[:, :2].reshape(-1), fields[:, -2:].reshape(-1),
        target_geom[:, :1].reshape(-1), target_geom[:, -1:].reshape(-1),
    ])
    got = copy_for_each(payload, "tile")
    src_rows = got[:, :n_src].reshape(n_tile, ROUNDS, 4, width)
    stacked = src_rows[owner, jnp.arange(ROUNDS)]
    rim = 2 * cols_here * 2
    above = from_peer(got[:, n_src:], row, -1, n_tile)
    below = from_peer(got[:, n_src:], row, 1, n_tile)
    f_above = above[rim:2 * rim].reshape(2, 2, cols_here)
    f_below = below[:rim].reshape(2, 2, cols_here)
    t_above = above[2 * rim + 6 * cols_here:].reshape(6, cols_here)
    t_below = below[2 * rim:2 * rim + 6 * cols_here].reshape(6, cols_here)
    ext_rows = jnp.concatenate([f_above, fields, f_below], axis=1)

    payload = jnp.concatenate([
        stacked.reshape(-1),
        ext_rows[:, :, :2].reshape(-1), ext_rows[:, :, -2:].reshape(-1),
        target_geom[:, :, 0].reshape(-1), target_geom[:, :, -1].reshape(-1),
    ])
    got = copy_for_each(payload, "eval")
    all_src = got[:, :n_src].reshape(n_eval, ROUNDS * 4, width)
    all_src = jnp.moveaxis(all_src, 0, 1).reshape(ROUNDS * 4, n_eval * width)
    rim = 2 * (rows_here + 4) * 2
    left = from_peer(got[:, n_src:], column, -1, n_eval)
    right = from_peer(got[:, n_src:], column, 1, n_eval)
    f_left = left[rim:2 * rim].reshape(2, rows_here + 4, 2)
    f_right = right[:rim].reshape(2, rows_here + 4, 2)
    t_left = left[2 * rim + 6 * rows_here:].reshape(6, rows_here)
    t_right = right[2 * rim:2 * rim + 6 * rows_here].reshape(6, rows_here)
    ext = jnp.concatenate([f_left, ext_rows, f_right], axis=2)

    sides = jnp.concatenate([t_left, t_right], axis=1)
    sides = jnp.pad(sides, ((0, 0), (0, cols_here - 2 * rows_here)))
    halo = jnp.stack([t_above, t_below, sides], axis=1)
    halo = jnp.pad(halo, ((0, 0), (0, rows_here - 3), (0, 0)))
    vel_all = velocity(group_len, all_src, jnp.concatenate([target_geom, halo], axis=1))
    vel_main = vel_all[:rows_here]
    vel_up = vel_all[rows_here:rows_here + 1]
    vel_down = vel_all[rows_here + 1:rows_here + 2]
    vel_left = vel_all[rows_here + 2, :rows_here][:, None]
    vel_right = vel_all[rows_here + 2, rows_here:2 * rows_here][:, None]

    vel_rows = jnp.concatenate([vel_up, vel_main, vel_down], axis=0)
    corner = jnp.zeros((1, 1), jnp.float32)
    vel_l = jnp.concatenate([corner, vel_left, corner], axis=0)
    vel_r = jnp.concatenate([corner, vel_right, corner], axis=0)
    vel = jnp.concatenate([vel_l, vel_rows, vel_r], axis=1)
    rates = tendency(ext, vel)
    row_ids = row * rows_here + jnp.arange(rows_here + 2, dtype=jnp.int32) - 1
    col_ids = column * cols_here + jnp.arange(cols_here + 2, dtype=jnp.int32) - 1
    row_ok = (row_ids >= 0) & (row_ids < rows_here * n_tile)
    col_ok = (col_ids >= 0) & (col_ids < cols_here * n_eval)
    inside = (row_ok[:, None] & col_ok[None, :]).astype(jnp.float32)
    smoothed = smooth(rates * inside[None])
    return (eta + 0.5 * smoothed[0], phi + 0.5 * smoothed[1], vel_main)


def solution(mesh):
    return jax.shard_map(
        body,
        mesh=mesh,
        in_specs=(
            P(None, "tile", "eval"),
            P("tile", "eval"),
            P("tile", "eval"),
            P("tile", None, None, "eval"),
            P(),
            P(),
        ),
        out_specs=(P("tile", "eval"), P("tile", "eval"), P("tile", "eval")),
        check_vma=False,
    )
```

```python
import functools

import jax
import jax.numpy as jnp
from jax import lax
from jax.experimental import pallas as pl
from jax.experimental.pallas import tpu as pltpu
from jax.sharding import PartitionSpec as P

ROUNDS = 4
SC = 32
CHUNK = 8

EPS2 = 0.05


def copy_for_each(x, axis):
    peers = lax.axis_size(axis)
    return lax.all_to_all(jnp.broadcast_to(x[None], (peers, *x.shape)), axis, 0, 0, tiled=True)


def from_peer(received, me, offset, peers):
    peer = me + offset
    ok = (peer >= 0) & (peer < peers)
    chunk = lax.dynamic_index_in_dim(received, jnp.clip(peer, 0, peers - 1), 0, keepdims=False)
    return jnp.where(ok, chunk, jnp.zeros_like(chunk))


def velocity_kernel(len_ref, src_ref, targ_ref, out_ref):
    tx, ty, tz = targ_ref[0], targ_ref[1], targ_ref[2]
    nx, ny, nz = targ_ref[3], targ_ref[4], targ_ref[5]
    per_column = ROUNDS * SC * 4

    def term(at, acc):
        sx = src_ref[at]
        sy = src_ref[at + 1]
        sz = src_ref[at + 2]
        q = src_ref[at + 3]
        dx = tx - sx
        dy = ty - sy
        dz = tz - sz
        dist2 = dx * dx + dy * dy + dz * dz + EPS2
        numer = nx * dx + ny * dy + nz * dz
        r = lax.rsqrt(dist2)
        return acc + (q * numer) * (r * r * r)

    acc = jnp.zeros(out_ref.shape, jnp.float32)
    for step in range(ROUNDS):

        def column(c, acc, step=step):
            chunks = (len_ref[step, c] + (CHUNK - 1)) // CHUNK
            start = c * per_column + step * SC * 4

            def chunk(j, acc):
                base = start + j * (CHUNK * 4)
                for u in range(CHUNK):
                    acc = term(base + 4 * u, acc)
                return acc

            return lax.fori_loop(0, chunks, chunk, acc)

        acc = lax.fori_loop(0, len_ref.shape[1], column, acc)
    out_ref[...] = acc


def velocity(group_len, src, targ):
    return pl.pallas_call(
        velocity_kernel,
        out_shape=jax.ShapeDtypeStruct(targ.shape[1:], jnp.float32),
        in_specs=[
            pl.BlockSpec(memory_space=pltpu.SMEM),
            pl.BlockSpec(memory_space=pltpu.SMEM),
            pl.BlockSpec(memory_space=pltpu.VMEM),
        ],
        out_specs=pl.BlockSpec(memory_space=pltpu.VMEM),
    )(group_len, src, targ)


def tendency(ext, vel):
    centre = ext[:, 1:-1, 1:-1]
    grad_x = (ext[:, 2:, 1:-1] - ext[:, :-2, 1:-1]) * 0.5
    grad_y = (ext[:, 1:-1, 2:] - ext[:, 1:-1, :-2]) * 0.5
    slope = 1.0 + grad_x[0] * grad_x[0] + grad_y[0] * grad_y[0]
    eta_rate = vel * slope - (grad_x[1] * grad_x[0] + grad_y[1] * grad_y[0])
    phi_rate = (
        -centre[0]
        - 0.5 * (grad_x[1] * grad_x[1] + grad_y[1] * grad_y[1])
        + 0.5 * vel * vel * slope
    )
    return jnp.stack([eta_rate, phi_rate])


def smooth(rim):
    centre = rim[:, 1:-1, 1:-1]
    return (
        4.0 * centre + rim[:, 2:, 1:-1] + rim[:, :-2, 1:-1] + rim[:, 1:-1, 2:] + rim[:, 1:-1, :-2]
    ) / 8.0


def body(target_geom, eta, phi, sources, group_len, owner):
    rows_here, cols_here = eta.shape
    n_tile, n_eval = lax.axis_size("tile"), lax.axis_size("eval")
    row = lax.axis_index("tile")
    column = lax.axis_index("eval")
    width = sources.shape[-1]
    group_len = group_len[:ROUNDS]
    owner = owner[:ROUNDS]

    fields = jnp.stack([eta, phi])
    n_src = ROUNDS * 4 * width
    payload = jnp.concatenate([
        jnp.swapaxes(sources[0], 1, 2).reshape(-1),
        fields[:, :2].reshape(-1), fields[:, -2:].reshape(-1),
        target_geom[:, :1].reshape(-1), target_geom[:, -1:].reshape(-1),
    ])
    got = copy_for_each(payload, "tile")
    src_rows = got[:, :n_src].reshape(n_tile, ROUNDS, width * 4)
    stacked = src_rows[owner, jnp.arange(ROUNDS)]
    rim = 2 * cols_here * 2
    above = from_peer(got[:, n_src:], row, -1, n_tile)
    below = from_peer(got[:, n_src:], row, 1, n_tile)
    f_above = above[rim:2 * rim].reshape(2, 2, cols_here)
    f_below = below[:rim].reshape(2, 2, cols_here)
    t_above = above[2 * rim + 6 * cols_here:].reshape(6, cols_here)
    t_below = below[2 * rim:2 * rim + 6 * cols_here].reshape(6, cols_here)
    ext_rows = jnp.concatenate([f_above, fields, f_below], axis=1)

    payload = jnp.concatenate([
        stacked.reshape(-1),
        ext_rows[:, :, :2].reshape(-1), ext_rows[:, :, -2:].reshape(-1),
        target_geom[:, :, 0].reshape(-1), target_geom[:, :, -1].reshape(-1),
    ])
    got = copy_for_each(payload, "eval")
    all_src = got[:, :n_src].reshape(n_eval, ROUNDS, width * 4)
    lane = jnp.arange(width * 4, dtype=jnp.int32)
    keep = ((lane % 4) != 3)[None, None, :] | ((lane // 4)[None, None, :] < group_len.T[:, :, None])
    all_src = jnp.where(keep, all_src, 0.0).reshape(-1)
    rim = 2 * (rows_here + 4) * 2
    left = from_peer(got[:, n_src:], column, -1, n_eval)
    right = from_peer(got[:, n_src:], column, 1, n_eval)
    f_left = left[rim:2 * rim].reshape(2, rows_here + 4, 2)
    f_right = right[:rim].reshape(2, rows_here + 4, 2)
    t_left = left[2 * rim + 6 * rows_here:].reshape(6, rows_here)
    t_right = right[2 * rim:2 * rim + 6 * rows_here].reshape(6, rows_here)
    ext = jnp.concatenate([f_left, ext_rows, f_right], axis=2)

    sides = jnp.concatenate([t_left, t_right], axis=1)
    sides = jnp.pad(sides, ((0, 0), (0, cols_here - 2 * rows_here)))
    halo = jnp.stack([t_above, t_below, sides], axis=1)
    halo = jnp.pad(halo, ((0, 0), (0, rows_here - 3), (0, 0)))
    vel_all = velocity(group_len, all_src, jnp.concatenate([target_geom, halo], axis=1))
    vel_main = vel_all[:rows_here]
    vel_up = vel_all[rows_here:rows_here + 1]
    vel_down = vel_all[rows_here + 1:rows_here + 2]
    vel_left = vel_all[rows_here + 2, :rows_here][:, None]
    vel_right = vel_all[rows_here + 2, rows_here:2 * rows_here][:, None]

    vel_rows = jnp.concatenate([vel_up, vel_main, vel_down], axis=0)
    corner = jnp.zeros((1, 1), jnp.float32)
    vel_l = jnp.concatenate([corner, vel_left, corner], axis=0)
    vel_r = jnp.concatenate([corner, vel_right, corner], axis=0)
    vel = jnp.concatenate([vel_l, vel_rows, vel_r], axis=1)
    rates = tendency(ext, vel)
    row_ids = row * rows_here + jnp.arange(rows_here + 2, dtype=jnp.int32) - 1
    col_ids = column * cols_here + jnp.arange(cols_here + 2, dtype=jnp.int32) - 1
    row_ok = (row_ids >= 0) & (row_ids < rows_here * n_tile)
    col_ok = (col_ids >= 0) & (col_ids < cols_here * n_eval)
    inside = (row_ok[:, None] & col_ok[None, :]).astype(jnp.float32)
    smoothed = smooth(rates * inside[None])
    return (eta + 0.5 * smoothed[0], phi + 0.5 * smoothed[1], vel_main)


def solution(mesh):
    return jax.shard_map(
        body,
        mesh=mesh,
        in_specs=(
            P(None, "tile", "eval"),
            P("tile", "eval"),
            P("tile", "eval"),
            P("tile", None, None, "eval"),
            P(),
            P(),
        ),
        out_specs=(P("tile", "eval"), P("tile", "eval"), P("tile", "eval")),
        check_vma=False,
    )
```

```python
import functools

import jax
import jax.numpy as jnp
from jax import lax
from jax.experimental import pallas as pl
from jax.experimental.pallas import tpu as pltpu
from jax.sharding import PartitionSpec as P

ROUNDS = 4
SC = 32
CHUNK = 8

EPS2 = 0.05


def copy_for_each(x, axis):
    peers = lax.axis_size(axis)
    return lax.all_to_all(jnp.broadcast_to(x[None], (peers, *x.shape)), axis, 0, 0, tiled=True)


def from_peer(received, me, offset, peers):
    peer = me + offset
    ok = (peer >= 0) & (peer < peers)
    chunk = lax.dynamic_index_in_dim(received, jnp.clip(peer, 0, peers - 1), 0, keepdims=False)
    return jnp.where(ok, chunk, jnp.zeros_like(chunk))


def velocity_kernel(len_ref, src_ref, targ_ref, out_ref):
    tx, ty, tz = targ_ref[0], targ_ref[1], targ_ref[2]
    nx, ny, nz = targ_ref[3], targ_ref[4], targ_ref[5]
    per_column = ROUNDS * SC * 4

    def term(at, acc):
        sx = src_ref[at]
        sy = src_ref[at + 1]
        sz = src_ref[at + 2]
        q = src_ref[at + 3]
        dx = tx - sx
        dy = ty - sy
        dz = tz - sz
        dist2 = dx * dx + dy * dy + dz * dz + EPS2
        numer = nx * dx + ny * dy + nz * dz
        r = lax.rsqrt(dist2)
        return acc + (q * numer) * (r * r * r)

    acc = jnp.zeros(out_ref.shape, jnp.float32)
    for step in range(ROUNDS):

        def column(c, acc, step=step):
            chunks = (len_ref[step, c] + (CHUNK - 1)) // CHUNK
            start = c * per_column + step * SC * 4

            def chunk(j, acc):
                base = start + j * (CHUNK * 4)
                for u in range(CHUNK):
                    acc = term(base + 4 * u, acc)
                return acc

            return lax.fori_loop(0, chunks, chunk, acc)

        acc = lax.fori_loop(0, len_ref.shape[1], column, acc)
    out_ref[...] = acc


def velocity(group_len, src, targ):
    return pl.pallas_call(
        velocity_kernel,
        out_shape=jax.ShapeDtypeStruct(targ.shape[1:], jnp.float32),
        in_specs=[
            pl.BlockSpec(memory_space=pltpu.SMEM),
            pl.BlockSpec(memory_space=pltpu.SMEM),
            pl.BlockSpec(memory_space=pltpu.VMEM),
        ],
        out_specs=pl.BlockSpec(memory_space=pltpu.VMEM),
    )(group_len, src, targ)


def halo_kernel(src_ref, targ_ref, out_ref):
    def group(g, carry):
        tx, ty, tz = targ_ref[g, 0], targ_ref[g, 1], targ_ref[g, 2]
        nx, ny, nz = targ_ref[g, 3], targ_ref[g, 4], targ_ref[g, 5]

        def chunk(j, acc):
            dx = tx - src_ref[0, j]
            dy = ty - src_ref[1, j]
            dz = tz - src_ref[2, j]
            dist2 = dx * dx + dy * dy + dz * dz + EPS2
            numer = nx * dx + ny * dy + nz * dz
            r = lax.rsqrt(dist2)
            return acc + (src_ref[3, j] * numer) * (r * r * r)

        out_ref[g] = lax.fori_loop(0, src_ref.shape[1], chunk, jnp.zeros(out_ref.shape[1:], jnp.float32),
                                   unroll=8)
        return carry

    lax.fori_loop(0, targ_ref.shape[0], group, 0)


def halo_velocity(src, targ):
    return pl.pallas_call(
        halo_kernel,
        out_shape=jax.ShapeDtypeStruct((targ.shape[0], 8, 128), jnp.float32),
        in_specs=[pl.BlockSpec(memory_space=pltpu.VMEM), pl.BlockSpec(memory_space=pltpu.VMEM)],
        out_specs=pl.BlockSpec(memory_space=pltpu.VMEM),
    )(src, targ)


def tendency(ext, vel):
    centre = ext[:, 1:-1, 1:-1]
    grad_x = (ext[:, 2:, 1:-1] - ext[:, :-2, 1:-1]) * 0.5
    grad_y = (ext[:, 1:-1, 2:] - ext[:, 1:-1, :-2]) * 0.5
    slope = 1.0 + grad_x[0] * grad_x[0] + grad_y[0] * grad_y[0]
    eta_rate = vel * slope - (grad_x[1] * grad_x[0] + grad_y[1] * grad_y[0])
    phi_rate = (
        -centre[0]
        - 0.5 * (grad_x[1] * grad_x[1] + grad_y[1] * grad_y[1])
        + 0.5 * vel * vel * slope
    )
    return jnp.stack([eta_rate, phi_rate])


def smooth(rim):
    centre = rim[:, 1:-1, 1:-1]
    return (
        4.0 * centre + rim[:, 2:, 1:-1] + rim[:, :-2, 1:-1] + rim[:, 1:-1, 2:] + rim[:, 1:-1, :-2]
    ) / 8.0


def body(target_geom, eta, phi, sources, group_len, owner):
    rows_here, cols_here = eta.shape
    n_tile, n_eval = lax.axis_size("tile"), lax.axis_size("eval")
    row = lax.axis_index("tile")
    column = lax.axis_index("eval")
    width = sources.shape[-1]
    group_len = group_len[:ROUNDS]
    owner = owner[:ROUNDS]

    fields = jnp.stack([eta, phi])
    n_src = ROUNDS * 4 * width
    payload = jnp.concatenate([
        jnp.swapaxes(sources[0], 1, 2).reshape(-1),
        fields[:, :2].reshape(-1), fields[:, -2:].reshape(-1),
        target_geom[:, :1].reshape(-1), target_geom[:, -1:].reshape(-1),
    ])
    got = copy_for_each(payload, "tile")
    src_rows = got[:, :n_src].reshape(n_tile, ROUNDS, width * 4)
    stacked = src_rows[owner, jnp.arange(ROUNDS)]
    rim = 2 * cols_here * 2
    above = from_peer(got[:, n_src:], row, -1, n_tile)
    below = from_peer(got[:, n_src:], row, 1, n_tile)
    f_above = above[rim:2 * rim].reshape(2, 2, cols_here)
    f_below = below[:rim].reshape(2, 2, cols_here)
    t_above = above[2 * rim + 6 * cols_here:].reshape(6, cols_here)
    t_below = below[2 * rim:2 * rim + 6 * cols_here].reshape(6, cols_here)
    ext_rows = jnp.concatenate([f_above, fields, f_below], axis=1)

    payload = jnp.concatenate([
        stacked.reshape(-1),
        ext_rows[:, :, :2].reshape(-1), ext_rows[:, :, -2:].reshape(-1),
        target_geom[:, :, 0].reshape(-1), target_geom[:, :, -1].reshape(-1),
    ])
    got = copy_for_each(payload, "eval")
    all_src = got[:, :n_src].reshape(n_eval, ROUNDS, width * 4)
    lane = jnp.arange(width * 4, dtype=jnp.int32)
    keep = ((lane % 4) != 3)[None, None, :] | ((lane // 4)[None, None, :] < group_len.T[:, :, None])
    all_src = jnp.where(keep, all_src, 0.0).reshape(-1)
    rim = 2 * (rows_here + 4) * 2
    left = from_peer(got[:, n_src:], column, -1, n_eval)
    right = from_peer(got[:, n_src:], column, 1, n_eval)
    f_left = left[rim:2 * rim].reshape(2, rows_here + 4, 2)
    f_right = right[:rim].reshape(2, rows_here + 4, 2)
    t_left = left[2 * rim + 6 * rows_here:].reshape(6, rows_here)
    t_right = right[2 * rim:2 * rim + 6 * rows_here].reshape(6, rows_here)
    ext = jnp.concatenate([f_left, ext_rows, f_right], axis=2)

    vel_main = velocity(group_len, all_src, target_geom)

    halo = jnp.concatenate([t_above, t_below, t_left, t_right], axis=1)
    n_halo = halo.shape[1]
    groups = n_halo // 8
    halo_t = jnp.broadcast_to(jnp.swapaxes(halo.reshape(6, groups, 8), 0, 1)[..., None], (groups, 6, 8, 128))
    src_t = all_src.reshape(-1, 4).T.reshape(4, -1, 1, 128)
    src_t = jnp.broadcast_to(src_t, (4, src_t.shape[1], 8, 128))
    vel_halo = halo_velocity(src_t, halo_t).sum(axis=-1).reshape(-1)
    vel_up = vel_halo[None, :cols_here]
    vel_down = vel_halo[None, cols_here:2 * cols_here]
    vel_left = vel_halo[2 * cols_here:2 * cols_here + rows_here][:, None]
    vel_right = vel_halo[2 * cols_here + rows_here:][:, None]

    vel_rows = jnp.concatenate([vel_up, vel_main, vel_down], axis=0)
    corner = jnp.zeros((1, 1), jnp.float32)
    vel_l = jnp.concatenate([corner, vel_left, corner], axis=0)
    vel_r = jnp.concatenate([corner, vel_right, corner], axis=0)
    vel = jnp.concatenate([vel_l, vel_rows, vel_r], axis=1)
    rates = tendency(ext, vel)
    row_ids = row * rows_here + jnp.arange(rows_here + 2, dtype=jnp.int32) - 1
    col_ids = column * cols_here + jnp.arange(cols_here + 2, dtype=jnp.int32) - 1
    row_ok = (row_ids >= 0) & (row_ids < rows_here * n_tile)
    col_ok = (col_ids >= 0) & (col_ids < cols_here * n_eval)
    inside = (row_ok[:, None] & col_ok[None, :]).astype(jnp.float32)
    smoothed = smooth(rates * inside[None])
    return (eta + 0.5 * smoothed[0], phi + 0.5 * smoothed[1], vel_main)


def solution(mesh):
    return jax.shard_map(
        body,
        mesh=mesh,
        in_specs=(
            P(None, "tile", "eval"),
            P("tile", "eval"),
            P("tile", "eval"),
            P("tile", None, None, "eval"),
            P(),
            P(),
        ),
        out_specs=(P("tile", "eval"), P("tile", "eval"), P("tile", "eval")),
        check_vma=False,
    )
```

```python
import functools

import jax
import jax.numpy as jnp
from jax import lax
from jax.experimental import pallas as pl
from jax.experimental.pallas import tpu as pltpu
from jax.sharding import PartitionSpec as P

ROUNDS = 4
SC = 32
CHUNK = 8

EPS2 = 0.05


def copy_for_each(x, axis):
    peers = lax.axis_size(axis)
    return lax.all_to_all(jnp.broadcast_to(x[None], (peers, *x.shape)), axis, 0, 0, tiled=True)


def from_peer(received, me, offset, peers):
    peer = me + offset
    ok = (peer >= 0) & (peer < peers)
    chunk = lax.dynamic_index_in_dim(received, jnp.clip(peer, 0, peers - 1), 0, keepdims=False)
    return jnp.where(ok, chunk, jnp.zeros_like(chunk))


def velocity_kernel(len_ref, src_ref, targ_ref, out_ref):
    tx, ty, tz = targ_ref[0], targ_ref[1], targ_ref[2]
    nx, ny, nz = targ_ref[3], targ_ref[4], targ_ref[5]
    per_column = ROUNDS * SC * 4

    def term(at, acc):
        sx = src_ref[at]
        sy = src_ref[at + 1]
        sz = src_ref[at + 2]
        q = src_ref[at + 3]
        dx = tx - sx
        dy = ty - sy
        dz = tz - sz
        dist2 = dx * dx + dy * dy + dz * dz + EPS2
        numer = nx * dx + ny * dy + nz * dz
        r = lax.rsqrt(dist2)
        return acc + (q * numer) * (r * r * r)

    def run(start, size):
        def block(j, acc):
            base = start + j * (size * 4)
            for u in range(size):
                acc = term(base + 4 * u, acc)
            return acc
        return block

    acc = jnp.zeros(out_ref.shape, jnp.float32)
    for step in range(ROUNDS):

        def column(c, acc, step=step):
            n = len_ref[step, c]
            eights = n // CHUNK
            pairs = eights // 2
            fours = (n - eights * CHUNK + 3) // 4
            start = c * per_column + step * SC * 4
            acc = lax.fori_loop(0, pairs, run(start, 2 * CHUNK), acc)
            acc = lax.fori_loop(pairs * 2, eights, run(start, CHUNK), acc)
            return lax.fori_loop(0, fours, run(start + eights * CHUNK * 4, 4), acc)

        acc = lax.fori_loop(0, len_ref.shape[1], column, acc)
    out_ref[...] = acc


def velocity(group_len, src, targ):
    return pl.pallas_call(
        velocity_kernel,
        out_shape=jax.ShapeDtypeStruct(targ.shape[1:], jnp.float32),
        in_specs=[
            pl.BlockSpec(memory_space=pltpu.SMEM),
            pl.BlockSpec(memory_space=pltpu.SMEM),
            pl.BlockSpec(memory_space=pltpu.VMEM),
        ],
        out_specs=pl.BlockSpec(memory_space=pltpu.VMEM),
    )(group_len, src, targ)


def tendency(ext, vel):
    centre = ext[:, 1:-1, 1:-1]
    grad_x = (ext[:, 2:, 1:-1] - ext[:, :-2, 1:-1]) * 0.5
    grad_y = (ext[:, 1:-1, 2:] - ext[:, 1:-1, :-2]) * 0.5
    slope = 1.0 + grad_x[0] * grad_x[0] + grad_y[0] * grad_y[0]
    eta_rate = vel * slope - (grad_x[1] * grad_x[0] + grad_y[1] * grad_y[0])
    phi_rate = (
        -centre[0]
        - 0.5 * (grad_x[1] * grad_x[1] + grad_y[1] * grad_y[1])
        + 0.5 * vel * vel * slope
    )
    return jnp.stack([eta_rate, phi_rate])


def smooth(rim):
    centre = rim[:, 1:-1, 1:-1]
    return (
        4.0 * centre + rim[:, 2:, 1:-1] + rim[:, :-2, 1:-1] + rim[:, 1:-1, 2:] + rim[:, 1:-1, :-2]
    ) / 8.0


def body(target_geom, eta, phi, sources, group_len, owner):
    rows_here, cols_here = eta.shape
    n_tile, n_eval = lax.axis_size("tile"), lax.axis_size("eval")
    row = lax.axis_index("tile")
    column = lax.axis_index("eval")
    width = sources.shape[-1]
    group_len = group_len[:ROUNDS]
    owner = owner[:ROUNDS]

    fields = jnp.stack([eta, phi])
    n_src = ROUNDS * 4 * width
    payload = jnp.concatenate([
        jnp.swapaxes(sources[0], 1, 2).reshape(-1),
        fields[:, :2].reshape(-1), fields[:, -2:].reshape(-1),
        target_geom[:, :1].reshape(-1), target_geom[:, -1:].reshape(-1),
    ])
    got = copy_for_each(payload, "tile")
    src_rows = got[:, :n_src].reshape(n_tile, ROUNDS, width * 4)
    stacked = src_rows[owner, jnp.arange(ROUNDS)]
    rim = 2 * cols_here * 2
    above = from_peer(got[:, n_src:], row, -1, n_tile)
    below = from_peer(got[:, n_src:], row, 1, n_tile)
    f_above = above[rim:2 * rim].reshape(2, 2, cols_here)
    f_below = below[:rim].reshape(2, 2, cols_here)
    t_above = above[2 * rim + 6 * cols_here:].reshape(6, cols_here)
    t_below = below[2 * rim:2 * rim + 6 * cols_here].reshape(6, cols_here)
    ext_rows = jnp.concatenate([f_above, fields, f_below], axis=1)

    payload = jnp.concatenate([
        stacked.reshape(-1),
        ext_rows[:, :, :2].reshape(-1), ext_rows[:, :, -2:].reshape(-1),
        target_geom[:, :, 0].reshape(-1), target_geom[:, :, -1].reshape(-1),
    ])
    got = copy_for_each(payload, "eval")
    all_src = got[:, :n_src].reshape(n_eval, ROUNDS, width * 4)
    lane = jnp.arange(width * 4, dtype=jnp.int32)
    keep = ((lane % 4) != 3)[None, None, :] | ((lane // 4)[None, None, :] < group_len.T[:, :, None])
    all_src = jnp.where(keep, all_src, 0.0).reshape(-1)
    rim = 2 * (rows_here + 4) * 2
    left = from_peer(got[:, n_src:], column, -1, n_eval)
    right = from_peer(got[:, n_src:], column, 1, n_eval)
    f_left = left[rim:2 * rim].reshape(2, rows_here + 4, 2)
    f_right = right[:rim].reshape(2, rows_here + 4, 2)
    t_left = left[2 * rim + 6 * rows_here:].reshape(6, rows_here)
    t_right = right[2 * rim:2 * rim + 6 * rows_here].reshape(6, rows_here)
    ext = jnp.concatenate([f_left, ext_rows, f_right], axis=2)

    sides = jnp.concatenate([t_left, t_right], axis=1)
    sides = jnp.pad(sides, ((0, 0), (0, cols_here - 2 * rows_here)))
    halo = jnp.stack([t_above, t_below, sides], axis=1)
    halo = jnp.pad(halo, ((0, 0), (0, rows_here - 3), (0, 0)))
    vel_all = velocity(group_len, all_src, jnp.concatenate([target_geom, halo], axis=1))
    vel_main = vel_all[:rows_here]
    vel_up = vel_all[rows_here:rows_here + 1]
    vel_down = vel_all[rows_here + 1:rows_here + 2]
    vel_left = vel_all[rows_here + 2, :rows_here][:, None]
    vel_right = vel_all[rows_here + 2, rows_here:2 * rows_here][:, None]

    vel_rows = jnp.concatenate([vel_up, vel_main, vel_down], axis=0)
    corner = jnp.zeros((1, 1), jnp.float32)
    vel_l = jnp.concatenate([corner, vel_left, corner], axis=0)
    vel_r = jnp.concatenate([corner, vel_right, corner], axis=0)
    vel = jnp.concatenate([vel_l, vel_rows, vel_r], axis=1)
    rates = tendency(ext, vel)
    row_ids = row * rows_here + jnp.arange(rows_here + 2, dtype=jnp.int32) - 1
    col_ids = column * cols_here + jnp.arange(cols_here + 2, dtype=jnp.int32) - 1
    row_ok = (row_ids >= 0) & (row_ids < rows_here * n_tile)
    col_ok = (col_ids >= 0) & (col_ids < cols_here * n_eval)
    inside = (row_ok[:, None] & col_ok[None, :]).astype(jnp.float32)
    smoothed = smooth(rates * inside[None])
    return (eta + 0.5 * smoothed[0], phi + 0.5 * smoothed[1], vel_main)


def solution(mesh):
    return jax.shard_map(
        body,
        mesh=mesh,
        in_specs=(
            P(None, "tile", "eval"),
            P("tile", "eval"),
            P("tile", "eval"),
            P("tile", None, None, "eval"),
            P(),
            P(),
        ),
        out_specs=(P("tile", "eval"), P("tile", "eval"), P("tile", "eval")),
        check_vma=False,
    )
```

```python
import functools

import jax
import jax.numpy as jnp
from jax import lax
from jax.experimental import pallas as pl
from jax.experimental.pallas import tpu as pltpu
from jax.sharding import PartitionSpec as P

ROUNDS = 4
SC = 32
BLOCK = 16

EPS2 = 0.05


def copy_for_each(x, axis):
    peers = lax.axis_size(axis)
    return lax.all_to_all(jnp.broadcast_to(x[None], (peers, *x.shape)), axis, 0, 0, tiled=True)


def from_peer(received, me, offset, peers):
    peer = me + offset
    ok = (peer >= 0) & (peer < peers)
    chunk = lax.dynamic_index_in_dim(received, jnp.clip(peer, 0, peers - 1), 0, keepdims=False)
    return jnp.where(ok, chunk, jnp.zeros_like(chunk))


def velocity_kernel(idx_ref, src_ref, targ_ref, out_ref):
    tx, ty, tz = targ_ref[0], targ_ref[1], targ_ref[2]
    nx, ny, nz = targ_ref[3], targ_ref[4], targ_ref[5]
    total = idx_ref[idx_ref.shape[0] - 1]

    def term(at, acc):
        sx = src_ref[at]
        sy = src_ref[at + 1]
        sz = src_ref[at + 2]
        q = src_ref[at + 3]
        dx = tx - sx
        dy = ty - sy
        dz = tz - sz
        dist2 = dx * dx + dy * dy + dz * dz + EPS2
        numer = nx * dx + ny * dy + nz * dz
        r = lax.rsqrt(dist2)
        return acc + (q * numer) * (r * r * r)

    def block(b, acc):
        first = b * BLOCK
        for u in range(BLOCK):
            acc = term(idx_ref[first + u] * 4, acc)
        return acc

    blocks = (total + (BLOCK - 1)) // BLOCK
    out_ref[...] = lax.fori_loop(0, blocks, block, jnp.zeros(out_ref.shape, jnp.float32))


def live_slots(group_len, slots):
    lengths = group_len.T.reshape(-1)
    ends = jnp.cumsum(lengths)
    at = jnp.arange(slots, dtype=jnp.int32)
    passed = ends[None, :] <= at[:, None]
    segment = jnp.sum(passed.astype(jnp.int32), axis=1)
    before = jnp.sum(jnp.where(passed, lengths[None, :], 0), axis=1)
    total = ends[-1]
    idx = jnp.where(at < total, segment * SC + (at - before), slots)
    return jnp.concatenate([idx, total[None]])


def velocity(idx, src, targ):
    return pl.pallas_call(
        velocity_kernel,
        out_shape=jax.ShapeDtypeStruct(targ.shape[1:], jnp.float32),
        in_specs=[
            pl.BlockSpec(memory_space=pltpu.SMEM),
            pl.BlockSpec(memory_space=pltpu.SMEM),
            pl.BlockSpec(memory_space=pltpu.VMEM),
        ],
        out_specs=pl.BlockSpec(memory_space=pltpu.VMEM),
    )(idx, src, targ)


def tendency(ext, vel):
    centre = ext[:, 1:-1, 1:-1]
    grad_x = (ext[:, 2:, 1:-1] - ext[:, :-2, 1:-1]) * 0.5
    grad_y = (ext[:, 1:-1, 2:] - ext[:, 1:-1, :-2]) * 0.5
    slope = 1.0 + grad_x[0] * grad_x[0] + grad_y[0] * grad_y[0]
    eta_rate = vel * slope - (grad_x[1] * grad_x[0] + grad_y[1] * grad_y[0])
    phi_rate = (
        -centre[0]
        - 0.5 * (grad_x[1] * grad_x[1] + grad_y[1] * grad_y[1])
        + 0.5 * vel * vel * slope
    )
    return jnp.stack([eta_rate, phi_rate])


def smooth(rim):
    centre = rim[:, 1:-1, 1:-1]
    return (
        4.0 * centre + rim[:, 2:, 1:-1] + rim[:, :-2, 1:-1] + rim[:, 1:-1, 2:] + rim[:, 1:-1, :-2]
    ) / 8.0


def body(target_geom, eta, phi, sources, group_len, owner):
    rows_here, cols_here = eta.shape
    n_tile, n_eval = lax.axis_size("tile"), lax.axis_size("eval")
    row = lax.axis_index("tile")
    column = lax.axis_index("eval")
    width = sources.shape[-1]
    group_len = group_len[:ROUNDS]
    owner = owner[:ROUNDS]

    fields = jnp.stack([eta, phi])
    n_src = ROUNDS * 4 * width
    payload = jnp.concatenate([
        jnp.swapaxes(sources[0], 1, 2).reshape(-1),
        fields[:, :2].reshape(-1), fields[:, -2:].reshape(-1),
        target_geom[:, :1].reshape(-1), target_geom[:, -1:].reshape(-1),
    ])
    got = copy_for_each(payload, "tile")
    src_rows = got[:, :n_src].reshape(n_tile, ROUNDS, width * 4)
    stacked = src_rows[owner, jnp.arange(ROUNDS)]
    rim = 2 * cols_here * 2
    above = from_peer(got[:, n_src:], row, -1, n_tile)
    below = from_peer(got[:, n_src:], row, 1, n_tile)
    f_above = above[rim:2 * rim].reshape(2, 2, cols_here)
    f_below = below[:rim].reshape(2, 2, cols_here)
    t_above = above[2 * rim + 6 * cols_here:].reshape(6, cols_here)
    t_below = below[2 * rim:2 * rim + 6 * cols_here].reshape(6, cols_here)
    ext_rows = jnp.concatenate([f_above, fields, f_below], axis=1)

    payload = jnp.concatenate([
        stacked.reshape(-1),
        ext_rows[:, :, :2].reshape(-1), ext_rows[:, :, -2:].reshape(-1),
        target_geom[:, :, 0].reshape(-1), target_geom[:, :, -1].reshape(-1),
    ])
    got = copy_for_each(payload, "eval")
    all_src = jnp.concatenate([got[:, :n_src].reshape(-1), jnp.zeros((4,), jnp.float32)])
    idx = live_slots(group_len, n_eval * ROUNDS * width)
    rim = 2 * (rows_here + 4) * 2
    left = from_peer(got[:, n_src:], column, -1, n_eval)
    right = from_peer(got[:, n_src:], column, 1, n_eval)
    f_left = left[rim:2 * rim].reshape(2, rows_here + 4, 2)
    f_right = right[:rim].reshape(2, rows_here + 4, 2)
    t_left = left[2 * rim + 6 * rows_here:].reshape(6, rows_here)
    t_right = right[2 * rim:2 * rim + 6 * rows_here].reshape(6, rows_here)
    ext = jnp.concatenate([f_left, ext_rows, f_right], axis=2)

    sides = jnp.concatenate([t_left, t_right], axis=1)
    sides = jnp.pad(sides, ((0, 0), (0, cols_here - 2 * rows_here)))
    halo = jnp.stack([t_above, t_below, sides], axis=1)
    halo = jnp.pad(halo, ((0, 0), (0, rows_here - 3), (0, 0)))
    vel_all = velocity(idx, all_src, jnp.concatenate([target_geom, halo], axis=1))
    vel_main = vel_all[:rows_here]
    vel_up = vel_all[rows_here:rows_here + 1]
    vel_down = vel_all[rows_here + 1:rows_here + 2]
    vel_left = vel_all[rows_here + 2, :rows_here][:, None]
    vel_right = vel_all[rows_here + 2, rows_here:2 * rows_here][:, None]

    vel_rows = jnp.concatenate([vel_up, vel_main, vel_down], axis=0)
    corner = jnp.zeros((1, 1), jnp.float32)
    vel_l = jnp.concatenate([corner, vel_left, corner], axis=0)
    vel_r = jnp.concatenate([corner, vel_right, corner], axis=0)
    vel = jnp.concatenate([vel_l, vel_rows, vel_r], axis=1)
    rates = tendency(ext, vel)
    row_ids = row * rows_here + jnp.arange(rows_here + 2, dtype=jnp.int32) - 1
    col_ids = column * cols_here + jnp.arange(cols_here + 2, dtype=jnp.int32) - 1
    row_ok = (row_ids >= 0) & (row_ids < rows_here * n_tile)
    col_ok = (col_ids >= 0) & (col_ids < cols_here * n_eval)
    inside = (row_ok[:, None] & col_ok[None, :]).astype(jnp.float32)
    smoothed = smooth(rates * inside[None])
    return (eta + 0.5 * smoothed[0], phi + 0.5 * smoothed[1], vel_main)


def solution(mesh):
    return jax.shard_map(
        body,
        mesh=mesh,
        in_specs=(
            P(None, "tile", "eval"),
            P("tile", "eval"),
            P("tile", "eval"),
            P("tile", None, None, "eval"),
            P(),
            P(),
        ),
        out_specs=(P("tile", "eval"), P("tile", "eval"), P("tile", "eval")),
        check_vma=False,
    )
```

```python
import functools

import jax
import jax.numpy as jnp
from jax import lax
from jax.experimental import pallas as pl
from jax.experimental.pallas import tpu as pltpu
from jax.sharding import PartitionSpec as P

ROUNDS = 4
SC = 32
BLOCK = 16

EPS2 = 0.05


def copy_for_each(x, axis):
    peers = lax.axis_size(axis)
    return lax.all_to_all(jnp.broadcast_to(x[None], (peers, *x.shape)), axis, 0, 0, tiled=True)


def from_peer(received, me, offset, peers):
    peer = me + offset
    ok = (peer >= 0) & (peer < peers)
    chunk = lax.dynamic_index_in_dim(received, jnp.clip(peer, 0, peers - 1), 0, keepdims=False)
    return jnp.where(ok, chunk, jnp.zeros_like(chunk))


def velocity_kernel(idx_ref, src_ref, main_ref, halo_ref, out_main_ref, out_halo_ref):
    tx = jnp.concatenate([main_ref[0], halo_ref[0]])
    ty = jnp.concatenate([main_ref[1], halo_ref[1]])
    tz = jnp.concatenate([main_ref[2], halo_ref[2]])
    nx = jnp.concatenate([main_ref[3], halo_ref[3]])
    ny = jnp.concatenate([main_ref[4], halo_ref[4]])
    nz = jnp.concatenate([main_ref[5], halo_ref[5]])
    total = idx_ref[idx_ref.shape[0] - 1]
    rows = main_ref.shape[1]

    def term(at, acc):
        sx = src_ref[at]
        sy = src_ref[at + SC]
        sz = src_ref[at + 2 * SC]
        q = src_ref[at + 3 * SC]
        dx = tx - sx
        dy = ty - sy
        dz = tz - sz
        dist2 = dx * dx + dy * dy + dz * dz + EPS2
        numer = nx * dx + ny * dy + nz * dz
        r = lax.rsqrt(dist2)
        return acc + (q * numer) * (r * r * r)

    def block(b, acc):
        first = b * BLOCK
        for u in range(BLOCK):
            acc = term(idx_ref[first + u], acc)
        return acc

    blocks = (total + (BLOCK - 1)) // BLOCK
    acc = lax.fori_loop(0, blocks, block, jnp.zeros((2 * rows, main_ref.shape[2]), jnp.float32))
    out_main_ref[...] = acc[:rows]
    out_halo_ref[...] = acc[rows:]


def live_slots(group_len, slots):
    lengths = group_len.T.reshape(-1)
    ends = jnp.cumsum(lengths)
    at = jnp.arange(slots, dtype=jnp.int32)
    passed = ends[None, :] <= at[:, None]
    segment = jnp.sum(passed.astype(jnp.int32), axis=1)
    before = jnp.sum(jnp.where(passed, lengths[None, :], 0), axis=1)
    total = ends[-1]
    idx = jnp.where(at < total, segment * (4 * SC) + (at - before), slots * 4)
    return jnp.concatenate([idx, total[None]])


def velocity(idx, src, main, halo):
    block = jax.ShapeDtypeStruct(main.shape[1:], jnp.float32)
    return pl.pallas_call(
        velocity_kernel,
        out_shape=(block, block),
        in_specs=[
            pl.BlockSpec(memory_space=pltpu.SMEM),
            pl.BlockSpec(memory_space=pltpu.SMEM),
            pl.BlockSpec(memory_space=pltpu.VMEM),
            pl.BlockSpec(memory_space=pltpu.VMEM),
        ],
        out_specs=(pl.BlockSpec(memory_space=pltpu.VMEM), pl.BlockSpec(memory_space=pltpu.VMEM)),
    )(idx, src, main, halo)


def tendency(ext, vel):
    centre = ext[:, 1:-1, 1:-1]
    grad_x = (ext[:, 2:, 1:-1] - ext[:, :-2, 1:-1]) * 0.5
    grad_y = (ext[:, 1:-1, 2:] - ext[:, 1:-1, :-2]) * 0.5
    slope = 1.0 + grad_x[0] * grad_x[0] + grad_y[0] * grad_y[0]
    eta_rate = vel * slope - (grad_x[1] * grad_x[0] + grad_y[1] * grad_y[0])
    phi_rate = (
        -centre[0]
        - 0.5 * (grad_x[1] * grad_x[1] + grad_y[1] * grad_y[1])
        + 0.5 * vel * vel * slope
    )
    return jnp.stack([eta_rate, phi_rate])


def smooth(rim):
    centre = rim[:, 1:-1, 1:-1]
    return (
        4.0 * centre + rim[:, 2:, 1:-1] + rim[:, :-2, 1:-1] + rim[:, 1:-1, 2:] + rim[:, 1:-1, :-2]
    ) / 8.0


def body(target_geom, eta, phi, sources, group_len, owner):
    rows_here, cols_here = eta.shape
    n_tile, n_eval = lax.axis_size("tile"), lax.axis_size("eval")
    row = lax.axis_index("tile")
    column = lax.axis_index("eval")
    width = sources.shape[-1]
    group_len = group_len[:ROUNDS]
    owner = owner[:ROUNDS]

    fields = jnp.stack([eta, phi])
    n_src = ROUNDS * 4 * width
    payload = jnp.concatenate([
        sources[0].reshape(-1),
        fields[:, :2].reshape(-1), fields[:, -2:].reshape(-1),
        target_geom[:, :1].reshape(-1), target_geom[:, -1:].reshape(-1),
    ])
    got = copy_for_each(payload, "tile")
    src_rows = got[:, :n_src].reshape(n_tile, ROUNDS, width * 4)
    stacked = src_rows[owner, jnp.arange(ROUNDS)]
    rim = 2 * cols_here * 2
    above = from_peer(got[:, n_src:], row, -1, n_tile)
    below = from_peer(got[:, n_src:], row, 1, n_tile)
    f_above = above[rim:2 * rim].reshape(2, 2, cols_here)
    f_below = below[:rim].reshape(2, 2, cols_here)
    t_above = above[2 * rim + 6 * cols_here:].reshape(6, cols_here)
    t_below = below[2 * rim:2 * rim + 6 * cols_here].reshape(6, cols_here)
    ext_rows = jnp.concatenate([f_above, fields, f_below], axis=1)

    payload = jnp.concatenate([
        stacked.reshape(-1),
        ext_rows[:, :, :2].reshape(-1), ext_rows[:, :, -2:].reshape(-1),
        target_geom[:, :, 0].reshape(-1), target_geom[:, :, -1].reshape(-1),
    ])
    got = copy_for_each(payload, "eval")
    all_src = jnp.concatenate([got[:, :n_src].reshape(-1), jnp.zeros((4 * SC,), jnp.float32)])
    idx = live_slots(group_len, n_eval * ROUNDS * width)
    rim = 2 * (rows_here + 4) * 2
    left = from_peer(got[:, n_src:], column, -1, n_eval)
    right = from_peer(got[:, n_src:], column, 1, n_eval)
    f_left = left[rim:2 * rim].reshape(2, rows_here + 4, 2)
    f_right = right[:rim].reshape(2, rows_here + 4, 2)
    t_left = left[2 * rim + 6 * rows_here:].reshape(6, rows_here)
    t_right = right[2 * rim:2 * rim + 6 * rows_here].reshape(6, rows_here)
    ext = jnp.concatenate([f_left, ext_rows, f_right], axis=2)

    sides = jnp.concatenate([t_left, t_right], axis=1)
    sides = jnp.pad(sides, ((0, 0), (0, cols_here - 2 * rows_here)))
    halo = jnp.stack([t_above, t_below, sides], axis=1)
    halo = jnp.pad(halo, ((0, 0), (0, rows_here - 3), (0, 0)))
    vel_main, vel_halo = velocity(idx, all_src, target_geom, halo)
    vel_up = vel_halo[0:1]
    vel_down = vel_halo[1:2]
    vel_left = vel_halo[2, :rows_here][:, None]
    vel_right = vel_halo[2, rows_here:2 * rows_here][:, None]

    vel_rows = jnp.concatenate([vel_up, vel_main, vel_down], axis=0)
    corner = jnp.zeros((1, 1), jnp.float32)
    vel_l = jnp.concatenate([corner, vel_left, corner], axis=0)
    vel_r = jnp.concatenate([corner, vel_right, corner], axis=0)
    vel = jnp.concatenate([vel_l, vel_rows, vel_r], axis=1)
    rates = tendency(ext, vel)
    row_ids = row * rows_here + jnp.arange(rows_here + 2, dtype=jnp.int32) - 1
    col_ids = column * cols_here + jnp.arange(cols_here + 2, dtype=jnp.int32) - 1
    row_ok = (row_ids >= 0) & (row_ids < rows_here * n_tile)
    col_ok = (col_ids >= 0) & (col_ids < cols_here * n_eval)
    inside = (row_ok[:, None] & col_ok[None, :]).astype(jnp.float32)
    smoothed = smooth(rates * inside[None])
    return (eta + 0.5 * smoothed[0], phi + 0.5 * smoothed[1], vel_main)


def solution(mesh):
    return jax.shard_map(
        body,
        mesh=mesh,
        in_specs=(
            P(None, "tile", "eval"),
            P("tile", "eval"),
            P("tile", "eval"),
            P("tile", None, None, "eval"),
            P(),
            P(),
        ),
        out_specs=(P("tile", "eval"), P("tile", "eval"), P("tile", "eval")),
        check_vma=False,
    )
```

```python
import functools

import jax
import jax.numpy as jnp
from jax import lax
from jax.experimental import pallas as pl
from jax.experimental.pallas import tpu as pltpu
from jax.sharding import PartitionSpec as P

ROUNDS = 4
SC = 32
BLOCK = 16

EPS2 = 0.05


def copy_for_each(x, axis):
    peers = lax.axis_size(axis)
    return lax.all_to_all(jnp.broadcast_to(x[None], (peers, *x.shape)), axis, 0, 0, tiled=True)


def from_peer(received, me, offset, peers):
    peer = me + offset
    ok = (peer >= 0) & (peer < peers)
    chunk = lax.dynamic_index_in_dim(received, jnp.clip(peer, 0, peers - 1), 0, keepdims=False)
    return jnp.where(ok, chunk, jnp.zeros_like(chunk))


def velocity_kernel(idx_ref, src_ref, main_ref, halo_ref, out_main_ref, out_halo_ref):
    tx = jnp.concatenate([main_ref[0], halo_ref[0]])
    ty = jnp.concatenate([main_ref[1], halo_ref[1]])
    tz = jnp.concatenate([main_ref[2], halo_ref[2]])
    nx = jnp.concatenate([main_ref[3], halo_ref[3]])
    ny = jnp.concatenate([main_ref[4], halo_ref[4]])
    nz = jnp.concatenate([main_ref[5], halo_ref[5]])
    total = idx_ref[idx_ref.shape[0] - 1]
    rows = main_ref.shape[1]

    def term(at, acc):
        sx = src_ref[at]
        sy = src_ref[at + SC]
        sz = src_ref[at + 2 * SC]
        q = src_ref[at + 3 * SC]
        dx = tx - sx
        dy = ty - sy
        dz = tz - sz
        dist2 = dx * dx + dy * dy + dz * dz + EPS2
        numer = nx * dx + ny * dy + nz * dz
        r = lax.rsqrt(dist2)
        return acc + (q * numer) * (r * r * r)

    def block(b, acc):
        first = b * BLOCK
        for u in range(BLOCK):
            acc = term(idx_ref[first + u], acc)
        return acc

    blocks = (total + (BLOCK - 1)) // BLOCK
    acc = lax.fori_loop(0, blocks, block, jnp.zeros((2 * rows, main_ref.shape[2]), jnp.float32))
    out_main_ref[...] = acc[:rows]
    out_halo_ref[...] = acc[rows:]


def live_slots(group_len, slots):
    lengths = group_len.T.reshape(-1)
    ends = jnp.cumsum(lengths)
    at = jnp.arange(slots, dtype=jnp.int32)
    passed = ends[None, :] <= at[:, None]
    segment = jnp.sum(passed.astype(jnp.int32), axis=1)
    before = jnp.sum(jnp.where(passed, lengths[None, :], 0), axis=1)
    total = ends[-1]
    idx = jnp.where(at < total, segment * (4 * SC) + (at - before), slots * 4)
    return jnp.concatenate([idx, total[None]])


def velocity(idx, src, main, halo):
    block = jax.ShapeDtypeStruct(main.shape[1:], jnp.float32)
    return pl.pallas_call(
        velocity_kernel,
        out_shape=(block, block),
        in_specs=[
            pl.BlockSpec(memory_space=pltpu.SMEM),
            pl.BlockSpec(memory_space=pltpu.SMEM),
            pl.BlockSpec(memory_space=pltpu.VMEM),
            pl.BlockSpec(memory_space=pltpu.VMEM),
        ],
        out_specs=(pl.BlockSpec(memory_space=pltpu.VMEM), pl.BlockSpec(memory_space=pltpu.VMEM)),
    )(idx, src, main, halo)


def tendency(ext, vel):
    centre = ext[:, 1:-1, 1:-1]
    grad_x = (ext[:, 2:, 1:-1] - ext[:, :-2, 1:-1]) * 0.5
    grad_y = (ext[:, 1:-1, 2:] - ext[:, 1:-1, :-2]) * 0.5
    slope = 1.0 + grad_x[0] * grad_x[0] + grad_y[0] * grad_y[0]
    eta_rate = vel * slope - (grad_x[1] * grad_x[0] + grad_y[1] * grad_y[0])
    phi_rate = (
        -centre[0]
        - 0.5 * (grad_x[1] * grad_x[1] + grad_y[1] * grad_y[1])
        + 0.5 * vel * vel * slope
    )
    return jnp.stack([eta_rate, phi_rate])


def smooth(rim):
    centre = rim[:, 1:-1, 1:-1]
    return (
        4.0 * centre + rim[:, 2:, 1:-1] + rim[:, :-2, 1:-1] + rim[:, 1:-1, 2:] + rim[:, 1:-1, :-2]
    ) / 8.0


def body(target_geom, eta, phi, sources, group_len, owner):
    rows_here, cols_here = eta.shape
    n_tile, n_eval = lax.axis_size("tile"), lax.axis_size("eval")
    row = lax.axis_index("tile")
    column = lax.axis_index("eval")
    width = sources.shape[-1]
    group_len = group_len[:ROUNDS]
    owner = owner[:ROUNDS]

    fields = jnp.stack([eta, phi])
    n_src = ROUNDS * 4 * width
    payload = jnp.concatenate([
        jnp.pad(sources[0].reshape(ROUNDS * 4, width), ((0, 0), (0, cols_here - width))),
        fields[:, :2].reshape(4, cols_here), fields[:, -2:].reshape(4, cols_here),
        target_geom[:, 0], target_geom[:, -1],
    ])
    got = copy_for_each(payload, "tile")
    src_rows = got[:, :ROUNDS * 4, :width].reshape(n_tile, ROUNDS, 4 * width)
    stacked = src_rows[owner, jnp.arange(ROUNDS)]
    above = from_peer(got, row, -1, n_tile)
    below = from_peer(got, row, 1, n_tile)
    top = ROUNDS * 4
    f_above = above[top + 4:top + 8].reshape(2, 2, cols_here)
    f_below = below[top:top + 4].reshape(2, 2, cols_here)
    t_above = above[top + 14:top + 20]
    t_below = below[top + 8:top + 14]
    ext_rows = jnp.concatenate([f_above, fields, f_below], axis=1)

    payload = jnp.concatenate([
        stacked.reshape(-1),
        ext_rows[:, :, :2].reshape(-1), ext_rows[:, :, -2:].reshape(-1),
        target_geom[:, :, 0].reshape(-1), target_geom[:, :, -1].reshape(-1),
    ])
    got = copy_for_each(payload, "eval")
    all_src = jnp.concatenate([got[:, :n_src].reshape(-1), jnp.zeros((4 * SC,), jnp.float32)])
    idx = live_slots(group_len, n_eval * ROUNDS * width)
    rim = 2 * (rows_here + 4) * 2
    left = from_peer(got[:, n_src:], column, -1, n_eval)
    right = from_peer(got[:, n_src:], column, 1, n_eval)
    f_left = left[rim:2 * rim].reshape(2, rows_here + 4, 2)
    f_right = right[:rim].reshape(2, rows_here + 4, 2)
    t_left = left[2 * rim + 6 * rows_here:].reshape(6, rows_here)
    t_right = right[2 * rim:2 * rim + 6 * rows_here].reshape(6, rows_here)
    ext = jnp.concatenate([f_left, ext_rows, f_right], axis=2)

    sides = jnp.concatenate([t_left, t_right], axis=1)
    sides = jnp.pad(sides, ((0, 0), (0, cols_here - 2 * rows_here)))
    halo = jnp.stack([t_above, t_below, sides], axis=1)
    halo = jnp.pad(halo, ((0, 0), (0, rows_here - 3), (0, 0)))
    vel_main, vel_halo = velocity(idx, all_src, target_geom, halo)
    vel_up = vel_halo[0:1]
    vel_down = vel_halo[1:2]
    vel_left = vel_halo[2, :rows_here][:, None]
    vel_right = vel_halo[2, rows_here:2 * rows_here][:, None]

    vel_rows = jnp.concatenate([vel_up, vel_main, vel_down], axis=0)
    corner = jnp.zeros((1, 1), jnp.float32)
    vel_l = jnp.concatenate([corner, vel_left, corner], axis=0)
    vel_r = jnp.concatenate([corner, vel_right, corner], axis=0)
    vel = jnp.concatenate([vel_l, vel_rows, vel_r], axis=1)
    rates = tendency(ext, vel)
    row_ids = row * rows_here + jnp.arange(rows_here + 2, dtype=jnp.int32) - 1
    col_ids = column * cols_here + jnp.arange(cols_here + 2, dtype=jnp.int32) - 1
    row_ok = (row_ids >= 0) & (row_ids < rows_here * n_tile)
    col_ok = (col_ids >= 0) & (col_ids < cols_here * n_eval)
    inside = (row_ok[:, None] & col_ok[None, :]).astype(jnp.float32)
    smoothed = smooth(rates * inside[None])
    return (eta + 0.5 * smoothed[0], phi + 0.5 * smoothed[1], vel_main)


def solution(mesh):
    return jax.shard_map(
        body,
        mesh=mesh,
        in_specs=(
            P(None, "tile", "eval"),
            P("tile", "eval"),
            P("tile", "eval"),
            P("tile", None, None, "eval"),
            P(),
            P(),
        ),
        out_specs=(P("tile", "eval"), P("tile", "eval"), P("tile", "eval")),
        check_vma=False,
    )
```

```python
import functools

import jax
import jax.numpy as jnp
from jax import lax
from jax.experimental import pallas as pl
from jax.experimental.pallas import tpu as pltpu
from jax.sharding import PartitionSpec as P

ROUNDS = 4
SC = 32
BLOCK = 16

EPS2 = 0.05


def copy_for_each(x, axis):
    peers = lax.axis_size(axis)
    return lax.all_to_all(jnp.broadcast_to(x[None], (peers, *x.shape)), axis, 0, 0, tiled=True)


def from_peer(received, me, offset, peers):
    peer = me + offset
    ok = (peer >= 0) & (peer < peers)
    chunk = lax.dynamic_index_in_dim(received, jnp.clip(peer, 0, peers - 1), 0, keepdims=False)
    return jnp.where(ok, chunk, jnp.zeros_like(chunk))


def velocity_kernel(idx_ref, src_ref, main_ref, halo_ref, out_main_ref, out_halo_ref):
    tx = jnp.concatenate([main_ref[0], halo_ref[0]])
    ty = jnp.concatenate([main_ref[1], halo_ref[1]])
    tz = jnp.concatenate([main_ref[2], halo_ref[2]])
    nx = jnp.concatenate([main_ref[3], halo_ref[3]])
    ny = jnp.concatenate([main_ref[4], halo_ref[4]])
    nz = jnp.concatenate([main_ref[5], halo_ref[5]])
    total = idx_ref[idx_ref.shape[0] - 1]
    rows = main_ref.shape[1]

    def term(at, acc):
        sx = src_ref[at]
        sy = src_ref[at + SC]
        sz = src_ref[at + 2 * SC]
        q = src_ref[at + 3 * SC]
        dx = tx - sx
        dy = ty - sy
        dz = tz - sz
        dist2 = dx * dx + dy * dy + dz * dz + EPS2
        numer = nx * dx + ny * dy + nz * dz
        r = lax.rsqrt(dist2)
        return acc + (q * numer) * (r * r * r)

    def block(b, acc):
        first = b * BLOCK
        for u in range(BLOCK):
            acc = term(idx_ref[first + u], acc)
        return acc

    blocks = (total + (BLOCK - 1)) // BLOCK
    acc = lax.fori_loop(0, blocks, block, jnp.zeros((2 * rows, main_ref.shape[2]), jnp.float32))
    out_main_ref[...] = acc[:rows]
    out_halo_ref[...] = acc[rows:]


def live_slots(group_len, slots):
    lengths = group_len.T.reshape(-1)
    ends = jnp.cumsum(lengths)
    at = jnp.arange(slots, dtype=jnp.int32)
    passed = ends[None, :] <= at[:, None]
    segment = jnp.sum(passed.astype(jnp.int32), axis=1)
    before = jnp.sum(jnp.where(passed, lengths[None, :], 0), axis=1)
    total = ends[-1]
    idx = jnp.where(at < total, segment * (4 * SC) + (at - before), slots * 4)
    return jnp.concatenate([idx, total[None]])


def velocity(idx, src, main, halo):
    block = jax.ShapeDtypeStruct(main.shape[1:], jnp.float32)
    return pl.pallas_call(
        velocity_kernel,
        out_shape=(block, block),
        in_specs=[
            pl.BlockSpec(memory_space=pltpu.SMEM),
            pl.BlockSpec(memory_space=pltpu.SMEM),
            pl.BlockSpec(memory_space=pltpu.VMEM),
            pl.BlockSpec(memory_space=pltpu.VMEM),
        ],
        out_specs=(pl.BlockSpec(memory_space=pltpu.VMEM), pl.BlockSpec(memory_space=pltpu.VMEM)),
    )(idx, src, main, halo)


def tendency(ext, vel):
    centre = ext[:, 1:-1, 1:-1]
    grad_x = (ext[:, 2:, 1:-1] - ext[:, :-2, 1:-1]) * 0.5
    grad_y = (ext[:, 1:-1, 2:] - ext[:, 1:-1, :-2]) * 0.5
    slope = 1.0 + grad_x[0] * grad_x[0] + grad_y[0] * grad_y[0]
    eta_rate = vel * slope - (grad_x[1] * grad_x[0] + grad_y[1] * grad_y[0])
    phi_rate = (
        -centre[0]
        - 0.5 * (grad_x[1] * grad_x[1] + grad_y[1] * grad_y[1])
        + 0.5 * vel * vel * slope
    )
    return jnp.stack([eta_rate, phi_rate])


def smooth(rim):
    centre = rim[:, 1:-1, 1:-1]
    return (
        4.0 * centre + rim[:, 2:, 1:-1] + rim[:, :-2, 1:-1] + rim[:, 1:-1, 2:] + rim[:, 1:-1, :-2]
    ) / 8.0


def body(target_geom, eta, phi, sources, group_len, owner):
    rows_here, cols_here = eta.shape
    n_tile, n_eval = lax.axis_size("tile"), lax.axis_size("eval")
    row = lax.axis_index("tile")
    column = lax.axis_index("eval")
    width = sources.shape[-1]
    group_len = group_len[:ROUNDS]
    owner = owner[:ROUNDS]

    fields = jnp.stack([eta, phi])
    mine = (owner == row).astype(jnp.float32)
    own_block = jnp.sum(mine[:, None, None] * sources[0], axis=0).reshape(-1)
    top = jnp.concatenate([fields[:, :2].reshape(-1), target_geom[:, 0].reshape(-1)])
    bottom = jnp.concatenate([fields[:, -2:].reshape(-1), target_geom[:, -1].reshape(-1)])
    to_above = (jnp.arange(n_tile, dtype=jnp.int32) == row - 1)[:, None]
    payload = jnp.concatenate([
        jnp.broadcast_to(own_block[None], (n_tile, own_block.shape[0])),
        jnp.where(to_above, top[None], bottom[None]),
    ], axis=1)
    got = lax.all_to_all(payload, "tile", 0, 0, tiled=True)
    n_own = own_block.shape[0]
    stacked = got[owner, :n_own]
    rim = 2 * cols_here * 2
    above = from_peer(got[:, n_own:], row, -1, n_tile)
    below = from_peer(got[:, n_own:], row, 1, n_tile)
    f_above = above[:rim].reshape(2, 2, cols_here)
    f_below = below[:rim].reshape(2, 2, cols_here)
    t_above = above[rim:].reshape(6, cols_here)
    t_below = below[rim:].reshape(6, cols_here)
    ext_rows = jnp.concatenate([f_above, fields, f_below], axis=1)

    n_src = ROUNDS * 4 * width
    left_rim = jnp.concatenate([ext_rows[:, :, :2].reshape(-1), target_geom[:, :, 0].reshape(-1)])
    right_rim = jnp.concatenate([ext_rows[:, :, -2:].reshape(-1), target_geom[:, :, -1].reshape(-1)])
    to_left = (jnp.arange(n_eval, dtype=jnp.int32) == column - 1)[:, None]
    payload = jnp.concatenate([
        jnp.broadcast_to(stacked.reshape(-1)[None], (n_eval, n_src)),
        jnp.where(to_left, left_rim[None], right_rim[None]),
    ], axis=1)
    got = lax.all_to_all(payload, "eval", 0, 0, tiled=True)
    all_src = jnp.concatenate([got[:, :n_src].reshape(-1), jnp.zeros((4 * SC,), jnp.float32)])
    idx = live_slots(group_len, n_eval * ROUNDS * width)
    rim = 2 * (rows_here + 4) * 2
    left = from_peer(got[:, n_src:], column, -1, n_eval)
    right = from_peer(got[:, n_src:], column, 1, n_eval)
    f_left = left[:rim].reshape(2, rows_here + 4, 2)
    f_right = right[:rim].reshape(2, rows_here + 4, 2)
    t_left = left[rim:].reshape(6, rows_here)
    t_right = right[rim:].reshape(6, rows_here)
    ext = jnp.concatenate([f_left, ext_rows, f_right], axis=2)

    sides = jnp.concatenate([t_left, t_right], axis=1)
    sides = jnp.pad(sides, ((0, 0), (0, cols_here - 2 * rows_here)))
    halo = jnp.stack([t_above, t_below, sides], axis=1)
    halo = jnp.pad(halo, ((0, 0), (0, rows_here - 3), (0, 0)))
    vel_main, vel_halo = velocity(idx, all_src, target_geom, halo)
    vel_up = vel_halo[0:1]
    vel_down = vel_halo[1:2]
    vel_left = vel_halo[2, :rows_here][:, None]
    vel_right = vel_halo[2, rows_here:2 * rows_here][:, None]

    vel_rows = jnp.concatenate([vel_up, vel_main, vel_down], axis=0)
    corner = jnp.zeros((1, 1), jnp.float32)
    vel_l = jnp.concatenate([corner, vel_left, corner], axis=0)
    vel_r = jnp.concatenate([corner, vel_right, corner], axis=0)
    vel = jnp.concatenate([vel_l, vel_rows, vel_r], axis=1)
    rates = tendency(ext, vel)
    row_ids = row * rows_here + jnp.arange(rows_here + 2, dtype=jnp.int32) - 1
    col_ids = column * cols_here + jnp.arange(cols_here + 2, dtype=jnp.int32) - 1
    row_ok = (row_ids >= 0) & (row_ids < rows_here * n_tile)
    col_ok = (col_ids >= 0) & (col_ids < cols_here * n_eval)
    inside = (row_ok[:, None] & col_ok[None, :]).astype(jnp.float32)
    smoothed = smooth(rates * inside[None])
    return (eta + 0.5 * smoothed[0], phi + 0.5 * smoothed[1], vel_main)


def solution(mesh):
    return jax.shard_map(
        body,
        mesh=mesh,
        in_specs=(
            P(None, "tile", "eval"),
            P("tile", "eval"),
            P("tile", "eval"),
            P("tile", None, None, "eval"),
            P(),
            P(),
        ),
        out_specs=(P("tile", "eval"), P("tile", "eval"), P("tile", "eval")),
        check_vma=False,
    )
```

```python
import functools

import jax
import jax.numpy as jnp
from jax import lax
from jax.experimental import pallas as pl
from jax.experimental.pallas import tpu as pltpu
from jax.sharding import PartitionSpec as P

ROUNDS = 4
SC = 32
BLOCK = 16

EPS2 = 0.05


def copy_for_each(x, axis):
    peers = lax.axis_size(axis)
    return lax.all_to_all(jnp.broadcast_to(x[None], (peers, *x.shape)), axis, 0, 0, tiled=True)


def from_peer(received, me, offset, peers):
    peer = me + offset
    ok = (peer >= 0) & (peer < peers)
    chunk = lax.dynamic_index_in_dim(received, jnp.clip(peer, 0, peers - 1), 0, keepdims=False)
    return jnp.where(ok, chunk, jnp.zeros_like(chunk))


def velocity_kernel(idx_ref, src_ref, main_ref, halo_ref, out_main_ref, out_halo_ref):
    tx = jnp.concatenate([main_ref[0], halo_ref[0]])
    ty = jnp.concatenate([main_ref[1], halo_ref[1]])
    tz = jnp.concatenate([main_ref[2], halo_ref[2]])
    nx = jnp.concatenate([main_ref[3], halo_ref[3]])
    ny = jnp.concatenate([main_ref[4], halo_ref[4]])
    nz = jnp.concatenate([main_ref[5], halo_ref[5]])
    total = idx_ref[idx_ref.shape[0] - 1]
    rows = main_ref.shape[1]

    def term(at, acc):
        sx = src_ref[at]
        sy = src_ref[at + SC]
        sz = src_ref[at + 2 * SC]
        q = src_ref[at + 3 * SC]
        dx = tx - sx
        dy = ty - sy
        dz = tz - sz
        dist2 = dx * dx + dy * dy + dz * dz + EPS2
        numer = nx * dx + ny * dy + nz * dz
        r = lax.rsqrt(dist2)
        return acc + (q * numer) * (r * r * r)

    def block(b, acc):
        first = b * BLOCK
        for u in range(BLOCK):
            acc = term(idx_ref[first + u], acc)
        return acc

    blocks = (total + (BLOCK - 1)) // BLOCK
    acc = lax.fori_loop(0, blocks, block, jnp.zeros((2 * rows, main_ref.shape[2]), jnp.float32))
    out_main_ref[...] = acc[:rows]
    out_halo_ref[...] = acc[rows:]


def live_slots(group_len, slots):
    lengths = group_len.T.reshape(-1)
    ends = jnp.cumsum(lengths)
    at = jnp.arange(slots, dtype=jnp.int32)
    passed = ends[None, :] <= at[:, None]
    segment = jnp.sum(passed.astype(jnp.int32), axis=1)
    before = jnp.sum(jnp.where(passed, lengths[None, :], 0), axis=1)
    total = ends[-1]
    idx = jnp.where(at < total, segment * (4 * SC) + (at - before), slots * 4)
    return jnp.concatenate([idx, total[None]])


def velocity(idx, src, main, halo):
    block = jax.ShapeDtypeStruct(main.shape[1:], jnp.float32)
    return pl.pallas_call(
        velocity_kernel,
        out_shape=(block, block),
        in_specs=[
            pl.BlockSpec(memory_space=pltpu.SMEM),
            pl.BlockSpec(memory_space=pltpu.SMEM),
            pl.BlockSpec(memory_space=pltpu.VMEM),
            pl.BlockSpec(memory_space=pltpu.VMEM),
        ],
        out_specs=(pl.BlockSpec(memory_space=pltpu.VMEM), pl.BlockSpec(memory_space=pltpu.VMEM)),
    )(idx, src, main, halo)


def tendency(ext, vel):
    centre = ext[:, 1:-1, 1:-1]
    grad_x = (ext[:, 2:, 1:-1] - ext[:, :-2, 1:-1]) * 0.5
    grad_y = (ext[:, 1:-1, 2:] - ext[:, 1:-1, :-2]) * 0.5
    slope = 1.0 + grad_x[0] * grad_x[0] + grad_y[0] * grad_y[0]
    eta_rate = vel * slope - (grad_x[1] * grad_x[0] + grad_y[1] * grad_y[0])
    phi_rate = (
        -centre[0]
        - 0.5 * (grad_x[1] * grad_x[1] + grad_y[1] * grad_y[1])
        + 0.5 * vel * vel * slope
    )
    return jnp.stack([eta_rate, phi_rate])


def smooth(rim):
    centre = rim[:, 1:-1, 1:-1]
    return (
        4.0 * centre + rim[:, 2:, 1:-1] + rim[:, :-2, 1:-1] + rim[:, 1:-1, 2:] + rim[:, 1:-1, :-2]
    ) / 8.0


def body(target_geom, eta, phi, sources, group_len, owner):
    rows_here, cols_here = eta.shape
    n_tile, n_eval = lax.axis_size("tile"), lax.axis_size("eval")
    row = lax.axis_index("tile")
    column = lax.axis_index("eval")
    width = sources.shape[-1]
    group_len = group_len[:ROUNDS]
    owner = owner[:ROUNDS]

    fields = jnp.stack([eta, phi])
    mine = (owner == row).astype(jnp.float32)
    own_block = jnp.sum(mine[:, None, None] * sources[0], axis=0).reshape(-1)
    top = jnp.concatenate([fields[:, :2].reshape(-1), target_geom[:, 0].reshape(-1)])
    bottom = jnp.concatenate([fields[:, -2:].reshape(-1), target_geom[:, -1].reshape(-1)])
    to_above = (jnp.arange(n_tile, dtype=jnp.int32) == row - 1)[:, None]
    payload = jnp.concatenate([
        jnp.broadcast_to(own_block[None], (n_tile, own_block.shape[0])),
        jnp.where(to_above, top[None], bottom[None]),
    ], axis=1)
    got = lax.all_to_all(payload, "tile", 0, 0, tiled=True)
    n_own = own_block.shape[0]
    stacked = got[:, :n_own][owner]
    rim = 2 * cols_here * 2
    above = from_peer(got[:, n_own:], row, -1, n_tile)
    below = from_peer(got[:, n_own:], row, 1, n_tile)
    f_above = above[:rim].reshape(2, 2, cols_here)
    f_below = below[:rim].reshape(2, 2, cols_here)
    t_above = above[rim:].reshape(6, cols_here)
    t_below = below[rim:].reshape(6, cols_here)
    ext_rows = jnp.concatenate([f_above, fields, f_below], axis=1)

    n_src = ROUNDS * 4 * width
    left_rim = jnp.concatenate([ext_rows[:, :, :2].reshape(-1), target_geom[:, :, 0].reshape(-1)])
    right_rim = jnp.concatenate([ext_rows[:, :, -2:].reshape(-1), target_geom[:, :, -1].reshape(-1)])
    to_left = (jnp.arange(n_eval, dtype=jnp.int32) == column - 1)[:, None]
    payload = jnp.concatenate([
        jnp.broadcast_to(stacked.reshape(-1)[None], (n_eval, n_src)),
        jnp.where(to_left, left_rim[None], right_rim[None]),
    ], axis=1)
    got = lax.all_to_all(payload, "eval", 0, 0, tiled=True)
    all_src = jnp.concatenate([got[:, :n_src].reshape(-1), jnp.zeros((4 * SC,), jnp.float32)])
    idx = live_slots(group_len, n_eval * ROUNDS * width)
    rim = 2 * (rows_here + 4) * 2
    left = from_peer(got[:, n_src:], column, -1, n_eval)
    right = from_peer(got[:, n_src:], column, 1, n_eval)
    f_left = left[:rim].reshape(2, rows_here + 4, 2)
    f_right = right[:rim].reshape(2, rows_here + 4, 2)
    t_left = left[rim:].reshape(6, rows_here)
    t_right = right[rim:].reshape(6, rows_here)
    ext = jnp.concatenate([f_left, ext_rows, f_right], axis=2)

    sides = jnp.concatenate([t_left, t_right], axis=1)
    sides = jnp.pad(sides, ((0, 0), (0, cols_here - 2 * rows_here)))
    halo = jnp.stack([t_above, t_below, sides], axis=1)
    halo = jnp.pad(halo, ((0, 0), (0, rows_here - 3), (0, 0)))
    vel_main, vel_halo = velocity(idx, all_src, target_geom, halo)
    vel_up = vel_halo[0:1]
    vel_down = vel_halo[1:2]
    vel_left = vel_halo[2, :rows_here][:, None]
    vel_right = vel_halo[2, rows_here:2 * rows_here][:, None]

    vel_rows = jnp.concatenate([vel_up, vel_main, vel_down], axis=0)
    corner = jnp.zeros((1, 1), jnp.float32)
    vel_l = jnp.concatenate([corner, vel_left, corner], axis=0)
    vel_r = jnp.concatenate([corner, vel_right, corner], axis=0)
    vel = jnp.concatenate([vel_l, vel_rows, vel_r], axis=1)
    rates = tendency(ext, vel)
    row_ids = row * rows_here + jnp.arange(rows_here + 2, dtype=jnp.int32) - 1
    col_ids = column * cols_here + jnp.arange(cols_here + 2, dtype=jnp.int32) - 1
    row_ok = (row_ids >= 0) & (row_ids < rows_here * n_tile)
    col_ok = (col_ids >= 0) & (col_ids < cols_here * n_eval)
    inside = (row_ok[:, None] & col_ok[None, :]).astype(jnp.float32)
    smoothed = smooth(rates * inside[None])
    return (eta + 0.5 * smoothed[0], phi + 0.5 * smoothed[1], vel_main)


def solution(mesh):
    return jax.shard_map(
        body,
        mesh=mesh,
        in_specs=(
            P(None, "tile", "eval"),
            P("tile", "eval"),
            P("tile", "eval"),
            P("tile", None, None, "eval"),
            P(),
            P(),
        ),
        out_specs=(P("tile", "eval"), P("tile", "eval"), P("tile", "eval")),
        check_vma=False,
    )
```

```python
import functools

import jax
import jax.numpy as jnp
from jax import lax
from jax.experimental import pallas as pl
from jax.experimental.pallas import tpu as pltpu
from jax.sharding import PartitionSpec as P

ROUNDS = 4
SC = 32
BLOCK = 16

EPS2 = 0.05


def copy_for_each(x, axis):
    peers = lax.axis_size(axis)
    return lax.all_to_all(jnp.broadcast_to(x[None], (peers, *x.shape)), axis, 0, 0, tiled=True)


def from_peer(received, me, offset, peers):
    peer = me + offset
    ok = (peer >= 0) & (peer < peers)
    chunk = lax.dynamic_index_in_dim(received, jnp.clip(peer, 0, peers - 1), 0, keepdims=False)
    return jnp.where(ok, chunk, jnp.zeros_like(chunk))


def velocity_kernel(idx_ref, src_ref, main_ref, halo_ref, out_main_ref, out_halo_ref):
    total = idx_ref[idx_ref.shape[0] - 1]
    main = tuple(main_ref[k] for k in range(6))
    halo = tuple(halo_ref[k] for k in range(6))
    upper = lax.broadcasted_iota(jnp.int32, main[0].shape, 0) < main[0].shape[0] // 2

    def load(at):
        return src_ref[at], src_ref[at + SC], src_ref[at + 2 * SC], src_ref[at + 3 * SC]

    def term(targ, src, acc):
        tx, ty, tz, nx, ny, nz = targ
        sx, sy, sz, q = src
        dx = tx - sx
        dy = ty - sy
        dz = tz - sz
        dist2 = dx * dx + dy * dy + dz * dz + EPS2
        numer = nx * dx + ny * dy + nz * dz
        r = lax.rsqrt(dist2)
        return acc + (q * numer) * (r * r * r)

    def block(b, accs):
        acc_m, acc_h = accs
        first = b * BLOCK
        for u in range(0, BLOCK, 2):
            one = load(idx_ref[first + u])
            two = load(idx_ref[first + u + 1])
            acc_m = term(main, one, acc_m)
            acc_m = term(main, two, acc_m)
            both = tuple(jnp.where(upper, x, y) for x, y in zip(one, two))
            acc_h = term(halo, both, acc_h)
        return acc_m, acc_h

    blocks = (total + (BLOCK - 1)) // BLOCK
    zero = jnp.zeros(main[0].shape, jnp.float32)
    acc_m, acc_h = lax.fori_loop(0, blocks, block, (zero, zero))
    half = acc_h.shape[0] // 2
    out_main_ref[...] = acc_m
    out_halo_ref[...] = acc_h[:half] + acc_h[half:]


def live_slots(group_len, slots):
    lengths = group_len.T.reshape(-1)
    ends = jnp.cumsum(lengths)
    at = jnp.arange(slots, dtype=jnp.int32)
    passed = ends[None, :] <= at[:, None]
    segment = jnp.sum(passed.astype(jnp.int32), axis=1)
    before = jnp.sum(jnp.where(passed, lengths[None, :], 0), axis=1)
    total = ends[-1]
    idx = jnp.where(at < total, segment * (4 * SC) + (at - before), slots * 4)
    return jnp.concatenate([idx, total[None]])


def velocity(idx, src, main, halo):
    half = jax.ShapeDtypeStruct((halo.shape[1] // 2, halo.shape[2]), jnp.float32)
    return pl.pallas_call(
        velocity_kernel,
        out_shape=(jax.ShapeDtypeStruct(main.shape[1:], jnp.float32), half),
        in_specs=[
            pl.BlockSpec(memory_space=pltpu.SMEM),
            pl.BlockSpec(memory_space=pltpu.SMEM),
            pl.BlockSpec(memory_space=pltpu.VMEM),
            pl.BlockSpec(memory_space=pltpu.VMEM),
        ],
        out_specs=(pl.BlockSpec(memory_space=pltpu.VMEM), pl.BlockSpec(memory_space=pltpu.VMEM)),
    )(idx, src, main, halo)


def tendency(ext, vel):
    centre = ext[:, 1:-1, 1:-1]
    grad_x = (ext[:, 2:, 1:-1] - ext[:, :-2, 1:-1]) * 0.5
    grad_y = (ext[:, 1:-1, 2:] - ext[:, 1:-1, :-2]) * 0.5
    slope = 1.0 + grad_x[0] * grad_x[0] + grad_y[0] * grad_y[0]
    eta_rate = vel * slope - (grad_x[1] * grad_x[0] + grad_y[1] * grad_y[0])
    phi_rate = (
        -centre[0]
        - 0.5 * (grad_x[1] * grad_x[1] + grad_y[1] * grad_y[1])
        + 0.5 * vel * vel * slope
    )
    return jnp.stack([eta_rate, phi_rate])


def smooth(rim):
    centre = rim[:, 1:-1, 1:-1]
    return (
        4.0 * centre + rim[:, 2:, 1:-1] + rim[:, :-2, 1:-1] + rim[:, 1:-1, 2:] + rim[:, 1:-1, :-2]
    ) / 8.0


def body(target_geom, eta, phi, sources, group_len, owner):
    rows_here, cols_here = eta.shape
    n_tile, n_eval = lax.axis_size("tile"), lax.axis_size("eval")
    row = lax.axis_index("tile")
    column = lax.axis_index("eval")
    width = sources.shape[-1]
    group_len = group_len[:ROUNDS]
    owner = owner[:ROUNDS]

    fields = jnp.stack([eta, phi])
    mine = (owner == row).astype(jnp.float32)
    own_block = jnp.sum(mine[:, None, None] * sources[0], axis=0).reshape(-1)
    top = jnp.concatenate([fields[:, :2].reshape(-1), target_geom[:, 0].reshape(-1)])
    bottom = jnp.concatenate([fields[:, -2:].reshape(-1), target_geom[:, -1].reshape(-1)])
    to_above = (jnp.arange(n_tile, dtype=jnp.int32) == row - 1)[:, None]
    payload = jnp.concatenate([
        jnp.broadcast_to(own_block[None], (n_tile, own_block.shape[0])),
        jnp.where(to_above, top[None], bottom[None]),
    ], axis=1)
    got = lax.all_to_all(payload, "tile", 0, 0, tiled=True)
    n_own = own_block.shape[0]
    stacked = got[:, :n_own][owner]
    rim = 2 * cols_here * 2
    above = from_peer(got[:, n_own:], row, -1, n_tile)
    below = from_peer(got[:, n_own:], row, 1, n_tile)
    f_above = above[:rim].reshape(2, 2, cols_here)
    f_below = below[:rim].reshape(2, 2, cols_here)
    t_above = above[rim:].reshape(6, cols_here)
    t_below = below[rim:].reshape(6, cols_here)
    ext_rows = jnp.concatenate([f_above, fields, f_below], axis=1)

    n_src = ROUNDS * 4 * width
    left_rim = jnp.concatenate([ext_rows[:, :, :2].reshape(-1), target_geom[:, :, 0].reshape(-1)])
    right_rim = jnp.concatenate([ext_rows[:, :, -2:].reshape(-1), target_geom[:, :, -1].reshape(-1)])
    to_left = (jnp.arange(n_eval, dtype=jnp.int32) == column - 1)[:, None]
    payload = jnp.concatenate([
        jnp.broadcast_to(stacked.reshape(-1)[None], (n_eval, n_src)),
        jnp.where(to_left, left_rim[None], right_rim[None]),
    ], axis=1)
    got = lax.all_to_all(payload, "eval", 0, 0, tiled=True)
    all_src = jnp.concatenate([got[:, :n_src].reshape(-1), jnp.zeros((4 * SC,), jnp.float32)])
    idx = live_slots(group_len, n_eval * ROUNDS * width)
    rim = 2 * (rows_here + 4) * 2
    left = from_peer(got[:, n_src:], column, -1, n_eval)
    right = from_peer(got[:, n_src:], column, 1, n_eval)
    f_left = left[:rim].reshape(2, rows_here + 4, 2)
    f_right = right[:rim].reshape(2, rows_here + 4, 2)
    t_left = left[rim:].reshape(6, rows_here)
    t_right = right[rim:].reshape(6, rows_here)
    ext = jnp.concatenate([f_left, ext_rows, f_right], axis=2)

    sides = jnp.concatenate([t_left, t_right], axis=1)
    sides = jnp.pad(sides, ((0, 0), (0, cols_here - 2 * rows_here)))
    halo = jnp.stack([t_above, t_below, sides, jnp.zeros_like(sides)], axis=1)
    halo = jnp.concatenate([halo, halo], axis=1)
    vel_main, vel_halo = velocity(idx, all_src, target_geom, halo)
    vel_up = vel_halo[0:1]
    vel_down = vel_halo[1:2]
    vel_left = vel_halo[2, :rows_here][:, None]
    vel_right = vel_halo[2, rows_here:2 * rows_here][:, None]

    vel_rows = jnp.concatenate([vel_up, vel_main, vel_down], axis=0)
    corner = jnp.zeros((1, 1), jnp.float32)
    vel_l = jnp.concatenate([corner, vel_left, corner], axis=0)
    vel_r = jnp.concatenate([corner, vel_right, corner], axis=0)
    vel = jnp.concatenate([vel_l, vel_rows, vel_r], axis=1)
    rates = tendency(ext, vel)
    row_ids = row * rows_here + jnp.arange(rows_here + 2, dtype=jnp.int32) - 1
    col_ids = column * cols_here + jnp.arange(cols_here + 2, dtype=jnp.int32) - 1
    row_ok = (row_ids >= 0) & (row_ids < rows_here * n_tile)
    col_ok = (col_ids >= 0) & (col_ids < cols_here * n_eval)
    inside = (row_ok[:, None] & col_ok[None, :]).astype(jnp.float32)
    smoothed = smooth(rates * inside[None])
    return (eta + 0.5 * smoothed[0], phi + 0.5 * smoothed[1], vel_main)


def solution(mesh):
    return jax.shard_map(
        body,
        mesh=mesh,
        in_specs=(
            P(None, "tile", "eval"),
            P("tile", "eval"),
            P("tile", "eval"),
            P("tile", None, None, "eval"),
            P(),
            P(),
        ),
        out_specs=(P("tile", "eval"), P("tile", "eval"), P("tile", "eval")),
        check_vma=False,
    )
```

```python
import functools

import jax
import jax.numpy as jnp
from jax import lax
from jax.experimental import pallas as pl
from jax.experimental.pallas import tpu as pltpu
from jax.sharding import PartitionSpec as P

ROUNDS = 4
SC = 32
BLOCK = 32

EPS2 = 0.05


def copy_for_each(x, axis):
    peers = lax.axis_size(axis)
    return lax.all_to_all(jnp.broadcast_to(x[None], (peers, *x.shape)), axis, 0, 0, tiled=True)


def from_peer(received, me, offset, peers):
    peer = me + offset
    ok = (peer >= 0) & (peer < peers)
    chunk = lax.dynamic_index_in_dim(received, jnp.clip(peer, 0, peers - 1), 0, keepdims=False)
    return jnp.where(ok, chunk, jnp.zeros_like(chunk))


def velocity_kernel(idx_ref, src_ref, main_ref, halo_ref, out_main_ref, out_halo_ref):
    total = idx_ref[idx_ref.shape[0] - 1]
    main = tuple(main_ref[k] for k in range(6))
    halo = tuple(halo_ref[k] for k in range(6))
    upper = lax.broadcasted_iota(jnp.int32, main[0].shape, 0) < main[0].shape[0] // 2

    def load(at):
        return src_ref[at], src_ref[at + SC], src_ref[at + 2 * SC], src_ref[at + 3 * SC]

    def term(targ, src, acc):
        tx, ty, tz, nx, ny, nz = targ
        sx, sy, sz, q = src
        dx = tx - sx
        dy = ty - sy
        dz = tz - sz
        dist2 = dx * dx + dy * dy + dz * dz + EPS2
        numer = nx * dx + ny * dy + nz * dz
        r = lax.rsqrt(dist2)
        return acc + (q * numer) * (r * r * r)

    def block(b, accs):
        acc_m, acc_h = accs
        first = b * BLOCK
        for u in range(0, BLOCK, 2):
            one = load(idx_ref[first + u])
            two = load(idx_ref[first + u + 1])
            acc_m = term(main, one, acc_m)
            acc_m = term(main, two, acc_m)
            both = tuple(jnp.where(upper, x, y) for x, y in zip(one, two))
            acc_h = term(halo, both, acc_h)
        return acc_m, acc_h

    blocks = (total + (BLOCK - 1)) // BLOCK
    zero = jnp.zeros(main[0].shape, jnp.float32)
    acc_m, acc_h = lax.fori_loop(0, blocks, block, (zero, zero))
    half = acc_h.shape[0] // 2
    out_main_ref[...] = acc_m
    out_halo_ref[...] = acc_h[:half] + acc_h[half:]


def live_slots(group_len, slots):
    lengths = group_len.T.reshape(-1)
    ends = jnp.cumsum(lengths)
    at = jnp.arange(slots, dtype=jnp.int32)
    passed = ends[None, :] <= at[:, None]
    segment = jnp.sum(passed.astype(jnp.int32), axis=1)
    before = jnp.sum(jnp.where(passed, lengths[None, :], 0), axis=1)
    total = ends[-1]
    idx = jnp.where(at < total, segment * (4 * SC) + (at - before), slots * 4)
    return jnp.concatenate([idx, total[None]])


def velocity(idx, src, main, halo):
    half = jax.ShapeDtypeStruct((halo.shape[1] // 2, halo.shape[2]), jnp.float32)
    return pl.pallas_call(
        velocity_kernel,
        out_shape=(jax.ShapeDtypeStruct(main.shape[1:], jnp.float32), half),
        in_specs=[
            pl.BlockSpec(memory_space=pltpu.SMEM),
            pl.BlockSpec(memory_space=pltpu.SMEM),
            pl.BlockSpec(memory_space=pltpu.VMEM),
            pl.BlockSpec(memory_space=pltpu.VMEM),
        ],
        out_specs=(pl.BlockSpec(memory_space=pltpu.VMEM), pl.BlockSpec(memory_space=pltpu.VMEM)),
    )(idx, src, main, halo)


def tendency(ext, vel):
    centre = ext[:, 1:-1, 1:-1]
    grad_x = (ext[:, 2:, 1:-1] - ext[:, :-2, 1:-1]) * 0.5
    grad_y = (ext[:, 1:-1, 2:] - ext[:, 1:-1, :-2]) * 0.5
    slope = 1.0 + grad_x[0] * grad_x[0] + grad_y[0] * grad_y[0]
    eta_rate = vel * slope - (grad_x[1] * grad_x[0] + grad_y[1] * grad_y[0])
    phi_rate = (
        -centre[0]
        - 0.5 * (grad_x[1] * grad_x[1] + grad_y[1] * grad_y[1])
        + 0.5 * vel * vel * slope
    )
    return jnp.stack([eta_rate, phi_rate])


def smooth(rim):
    centre = rim[:, 1:-1, 1:-1]
    return (
        4.0 * centre + rim[:, 2:, 1:-1] + rim[:, :-2, 1:-1] + rim[:, 1:-1, 2:] + rim[:, 1:-1, :-2]
    ) / 8.0


def body(target_geom, eta, phi, sources, group_len, owner):
    rows_here, cols_here = eta.shape
    n_tile, n_eval = lax.axis_size("tile"), lax.axis_size("eval")
    row = lax.axis_index("tile")
    column = lax.axis_index("eval")
    width = sources.shape[-1]
    group_len = group_len[:ROUNDS]
    owner = owner[:ROUNDS]

    fields = jnp.stack([eta, phi])
    mine = (owner == row).astype(jnp.float32)
    own_block = jnp.sum(mine[:, None, None] * sources[0], axis=0).reshape(-1)
    top = jnp.concatenate([fields[:, :2].reshape(-1), target_geom[:, 0].reshape(-1)])
    bottom = jnp.concatenate([fields[:, -2:].reshape(-1), target_geom[:, -1].reshape(-1)])
    to_above = (jnp.arange(n_tile, dtype=jnp.int32) == row - 1)[:, None]
    payload = jnp.concatenate([
        jnp.broadcast_to(own_block[None], (n_tile, own_block.shape[0])),
        jnp.where(to_above, top[None], bottom[None]),
    ], axis=1)
    got = lax.all_to_all(payload, "tile", 0, 0, tiled=True)
    n_own = own_block.shape[0]
    stacked = got[:, :n_own][owner]
    rim = 2 * cols_here * 2
    above = from_peer(got[:, n_own:], row, -1, n_tile)
    below = from_peer(got[:, n_own:], row, 1, n_tile)
    f_above = above[:rim].reshape(2, 2, cols_here)
    f_below = below[:rim].reshape(2, 2, cols_here)
    t_above = above[rim:].reshape(6, cols_here)
    t_below = below[rim:].reshape(6, cols_here)
    ext_rows = jnp.concatenate([f_above, fields, f_below], axis=1)

    n_src = ROUNDS * 4 * width
    left_rim = jnp.concatenate([ext_rows[:, :, :2].reshape(-1), target_geom[:, :, 0].reshape(-1)])
    right_rim = jnp.concatenate([ext_rows[:, :, -2:].reshape(-1), target_geom[:, :, -1].reshape(-1)])
    to_left = (jnp.arange(n_eval, dtype=jnp.int32) == column - 1)[:, None]
    payload = jnp.concatenate([
        jnp.broadcast_to(stacked.reshape(-1)[None], (n_eval, n_src)),
        jnp.where(to_left, left_rim[None], right_rim[None]),
    ], axis=1)
    got = lax.all_to_all(payload, "eval", 0, 0, tiled=True)
    all_src = jnp.concatenate([got[:, :n_src].reshape(-1), jnp.zeros((4 * SC,), jnp.float32)])
    idx = live_slots(group_len, n_eval * ROUNDS * width)
    rim = 2 * (rows_here + 4) * 2
    left = from_peer(got[:, n_src:], column, -1, n_eval)
    right = from_peer(got[:, n_src:], column, 1, n_eval)
    f_left = left[:rim].reshape(2, rows_here + 4, 2)
    f_right = right[:rim].reshape(2, rows_here + 4, 2)
    t_left = left[rim:].reshape(6, rows_here)
    t_right = right[rim:].reshape(6, rows_here)
    ext = jnp.concatenate([f_left, ext_rows, f_right], axis=2)

    sides = jnp.concatenate([t_left, t_right], axis=1)
    sides = jnp.pad(sides, ((0, 0), (0, cols_here - 2 * rows_here)))
    halo = jnp.stack([t_above, t_below, sides, jnp.zeros_like(sides)], axis=1)
    halo = jnp.concatenate([halo, halo], axis=1)
    vel_main, vel_halo = velocity(idx, all_src, target_geom, halo)
    vel_up = vel_halo[0:1]
    vel_down = vel_halo[1:2]
    vel_left = vel_halo[2, :rows_here][:, None]
    vel_right = vel_halo[2, rows_here:2 * rows_here][:, None]

    vel_rows = jnp.concatenate([vel_up, vel_main, vel_down], axis=0)
    corner = jnp.zeros((1, 1), jnp.float32)
    vel_l = jnp.concatenate([corner, vel_left, corner], axis=0)
    vel_r = jnp.concatenate([corner, vel_right, corner], axis=0)
    vel = jnp.concatenate([vel_l, vel_rows, vel_r], axis=1)
    rates = tendency(ext, vel)
    row_ids = row * rows_here + jnp.arange(rows_here + 2, dtype=jnp.int32) - 1
    col_ids = column * cols_here + jnp.arange(cols_here + 2, dtype=jnp.int32) - 1
    row_ok = (row_ids >= 0) & (row_ids < rows_here * n_tile)
    col_ok = (col_ids >= 0) & (col_ids < cols_here * n_eval)
    inside = (row_ok[:, None] & col_ok[None, :]).astype(jnp.float32)
    smoothed = smooth(rates * inside[None])
    return (eta + 0.5 * smoothed[0], phi + 0.5 * smoothed[1], vel_main)


def solution(mesh):
    return jax.shard_map(
        body,
        mesh=mesh,
        in_specs=(
            P(None, "tile", "eval"),
            P("tile", "eval"),
            P("tile", "eval"),
            P("tile", None, None, "eval"),
            P(),
            P(),
        ),
        out_specs=(P("tile", "eval"), P("tile", "eval"), P("tile", "eval")),
        check_vma=False,
    )
```

```python
import functools

import jax
import jax.numpy as jnp
from jax import lax
from jax.experimental import pallas as pl
from jax.experimental.pallas import tpu as pltpu
from jax.sharding import PartitionSpec as P

ROUNDS = 4
SC = 32
BLOCK = 64

EPS2 = 0.05


def copy_for_each(x, axis):
    peers = lax.axis_size(axis)
    return lax.all_to_all(jnp.broadcast_to(x[None], (peers, *x.shape)), axis, 0, 0, tiled=True)


def from_peer(received, me, offset, peers):
    peer = me + offset
    ok = (peer >= 0) & (peer < peers)
    chunk = lax.dynamic_index_in_dim(received, jnp.clip(peer, 0, peers - 1), 0, keepdims=False)
    return jnp.where(ok, chunk, jnp.zeros_like(chunk))


def velocity_kernel(idx_ref, src_ref, main_ref, halo_ref, out_main_ref, out_halo_ref):
    total = idx_ref[idx_ref.shape[0] - 1]
    main = tuple(main_ref[k] for k in range(6))
    halo = tuple(halo_ref[k] for k in range(6))
    upper = lax.broadcasted_iota(jnp.int32, main[0].shape, 0) < main[0].shape[0] // 2

    def load(at):
        return src_ref[at], src_ref[at + SC], src_ref[at + 2 * SC], src_ref[at + 3 * SC]

    def term(targ, src, acc):
        tx, ty, tz, nx, ny, nz = targ
        sx, sy, sz, q = src
        dx = tx - sx
        dy = ty - sy
        dz = tz - sz
        dist2 = dx * dx + dy * dy + dz * dz + EPS2
        numer = nx * dx + ny * dy + nz * dz
        r = lax.rsqrt(dist2)
        return acc + (q * numer) * (r * r * r)

    def block(b, accs):
        acc_m, acc_h = accs
        first = b * BLOCK
        for u in range(0, BLOCK, 2):
            one = load(idx_ref[first + u])
            two = load(idx_ref[first + u + 1])
            acc_m = term(main, one, acc_m)
            acc_m = term(main, two, acc_m)
            both = tuple(jnp.where(upper, x, y) for x, y in zip(one, two))
            acc_h = term(halo, both, acc_h)
        return acc_m, acc_h

    blocks = (total + (BLOCK - 1)) // BLOCK
    zero = jnp.zeros(main[0].shape, jnp.float32)
    acc_m, acc_h = lax.fori_loop(0, blocks, block, (zero, zero))
    half = acc_h.shape[0] // 2
    out_main_ref[...] = acc_m
    out_halo_ref[...] = acc_h[:half] + acc_h[half:]


def live_slots(group_len, slots):
    lengths = group_len.T.reshape(-1)
    ends = jnp.cumsum(lengths)
    at = jnp.arange(slots, dtype=jnp.int32)
    passed = ends[None, :] <= at[:, None]
    segment = jnp.sum(passed.astype(jnp.int32), axis=1)
    before = jnp.sum(jnp.where(passed, lengths[None, :], 0), axis=1)
    total = ends[-1]
    idx = jnp.where(at < total, segment * (4 * SC) + (at - before), slots * 4)
    return jnp.concatenate([idx, total[None]])


def velocity(idx, src, main, halo):
    half = jax.ShapeDtypeStruct((halo.shape[1] // 2, halo.shape[2]), jnp.float32)
    return pl.pallas_call(
        velocity_kernel,
        out_shape=(jax.ShapeDtypeStruct(main.shape[1:], jnp.float32), half),
        in_specs=[
            pl.BlockSpec(memory_space=pltpu.SMEM),
            pl.BlockSpec(memory_space=pltpu.SMEM),
            pl.BlockSpec(memory_space=pltpu.VMEM),
            pl.BlockSpec(memory_space=pltpu.VMEM),
        ],
        out_specs=(pl.BlockSpec(memory_space=pltpu.VMEM), pl.BlockSpec(memory_space=pltpu.VMEM)),
    )(idx, src, main, halo)


def tendency(ext, vel):
    centre = ext[:, 1:-1, 1:-1]
    grad_x = (ext[:, 2:, 1:-1] - ext[:, :-2, 1:-1]) * 0.5
    grad_y = (ext[:, 1:-1, 2:] - ext[:, 1:-1, :-2]) * 0.5
    slope = 1.0 + grad_x[0] * grad_x[0] + grad_y[0] * grad_y[0]
    eta_rate = vel * slope - (grad_x[1] * grad_x[0] + grad_y[1] * grad_y[0])
    phi_rate = (
        -centre[0]
        - 0.5 * (grad_x[1] * grad_x[1] + grad_y[1] * grad_y[1])
        + 0.5 * vel * vel * slope
    )
    return jnp.stack([eta_rate, phi_rate])


def smooth(rim):
    centre = rim[:, 1:-1, 1:-1]
    return (
        4.0 * centre + rim[:, 2:, 1:-1] + rim[:, :-2, 1:-1] + rim[:, 1:-1, 2:] + rim[:, 1:-1, :-2]
    ) / 8.0


def body(target_geom, eta, phi, sources, group_len, owner):
    rows_here, cols_here = eta.shape
    n_tile, n_eval = lax.axis_size("tile"), lax.axis_size("eval")
    row = lax.axis_index("tile")
    column = lax.axis_index("eval")
    width = sources.shape[-1]
    group_len = group_len[:ROUNDS]
    owner = owner[:ROUNDS]

    fields = jnp.stack([eta, phi])
    mine = (owner == row).astype(jnp.float32)
    own_block = jnp.sum(mine[:, None, None] * sources[0], axis=0).reshape(-1)
    top = jnp.concatenate([fields[:, :2].reshape(-1), target_geom[:, 0].reshape(-1)])
    bottom = jnp.concatenate([fields[:, -2:].reshape(-1), target_geom[:, -1].reshape(-1)])
    to_above = (jnp.arange(n_tile, dtype=jnp.int32) == row - 1)[:, None]
    payload = jnp.concatenate([
        jnp.broadcast_to(own_block[None], (n_tile, own_block.shape[0])),
        jnp.where(to_above, top[None], bottom[None]),
    ], axis=1)
    got = lax.all_to_all(payload, "tile", 0, 0, tiled=True)
    n_own = own_block.shape[0]
    stacked = got[:, :n_own][owner]
    rim = 2 * cols_here * 2
    above = from_peer(got[:, n_own:], row, -1, n_tile)
    below = from_peer(got[:, n_own:], row, 1, n_tile)
    f_above = above[:rim].reshape(2, 2, cols_here)
    f_below = below[:rim].reshape(2, 2, cols_here)
    t_above = above[rim:].reshape(6, cols_here)
    t_below = below[rim:].reshape(6, cols_here)
    ext_rows = jnp.concatenate([f_above, fields, f_below], axis=1)

    n_src = ROUNDS * 4 * width
    left_rim = jnp.concatenate([ext_rows[:, :, :2].reshape(-1), target_geom[:, :, 0].reshape(-1)])
    right_rim = jnp.concatenate([ext_rows[:, :, -2:].reshape(-1), target_geom[:, :, -1].reshape(-1)])
    to_left = (jnp.arange(n_eval, dtype=jnp.int32) == column - 1)[:, None]
    payload = jnp.concatenate([
        jnp.broadcast_to(stacked.reshape(-1)[None], (n_eval, n_src)),
        jnp.where(to_left, left_rim[None], right_rim[None]),
    ], axis=1)
    got = lax.all_to_all(payload, "eval", 0, 0, tiled=True)
    all_src = jnp.concatenate([got[:, :n_src].reshape(-1), jnp.zeros((4 * SC,), jnp.float32)])
    idx = live_slots(group_len, n_eval * ROUNDS * width)
    rim = 2 * (rows_here + 4) * 2
    left = from_peer(got[:, n_src:], column, -1, n_eval)
    right = from_peer(got[:, n_src:], column, 1, n_eval)
    f_left = left[:rim].reshape(2, rows_here + 4, 2)
    f_right = right[:rim].reshape(2, rows_here + 4, 2)
    t_left = left[rim:].reshape(6, rows_here)
    t_right = right[rim:].reshape(6, rows_here)
    ext = jnp.concatenate([f_left, ext_rows, f_right], axis=2)

    sides = jnp.concatenate([t_left, t_right], axis=1)
    sides = jnp.pad(sides, ((0, 0), (0, cols_here - 2 * rows_here)))
    halo = jnp.stack([t_above, t_below, sides, jnp.zeros_like(sides)], axis=1)
    halo = jnp.concatenate([halo, halo], axis=1)
    vel_main, vel_halo = velocity(idx, all_src, target_geom, halo)
    vel_up = vel_halo[0:1]
    vel_down = vel_halo[1:2]
    vel_left = vel_halo[2, :rows_here][:, None]
    vel_right = vel_halo[2, rows_here:2 * rows_here][:, None]

    vel_rows = jnp.concatenate([vel_up, vel_main, vel_down], axis=0)
    corner = jnp.zeros((1, 1), jnp.float32)
    vel_l = jnp.concatenate([corner, vel_left, corner], axis=0)
    vel_r = jnp.concatenate([corner, vel_right, corner], axis=0)
    vel = jnp.concatenate([vel_l, vel_rows, vel_r], axis=1)
    rates = tendency(ext, vel)
    row_ids = row * rows_here + jnp.arange(rows_here + 2, dtype=jnp.int32) - 1
    col_ids = column * cols_here + jnp.arange(cols_here + 2, dtype=jnp.int32) - 1
    row_ok = (row_ids >= 0) & (row_ids < rows_here * n_tile)
    col_ok = (col_ids >= 0) & (col_ids < cols_here * n_eval)
    inside = (row_ok[:, None] & col_ok[None, :]).astype(jnp.float32)
    smoothed = smooth(rates * inside[None])
    return (eta + 0.5 * smoothed[0], phi + 0.5 * smoothed[1], vel_main)


def solution(mesh):
    return jax.shard_map(
        body,
        mesh=mesh,
        in_specs=(
            P(None, "tile", "eval"),
            P("tile", "eval"),
            P("tile", "eval"),
            P("tile", None, None, "eval"),
            P(),
            P(),
        ),
        out_specs=(P("tile", "eval"), P("tile", "eval"), P("tile", "eval")),
        check_vma=False,
    )
```

```python
import functools

import jax
import jax.numpy as jnp
from jax import lax
from jax.experimental import pallas as pl
from jax.experimental.pallas import tpu as pltpu
from jax.sharding import PartitionSpec as P

ROUNDS = 4
SC = 32
BLOCK = 64

EPS2 = 0.05


def copy_for_each(x, axis):
    peers = lax.axis_size(axis)
    return lax.all_to_all(jnp.broadcast_to(x[None], (peers, *x.shape)), axis, 0, 0, tiled=True)


def from_peer(received, me, offset, peers):
    peer = me + offset
    ok = (peer >= 0) & (peer < peers)
    chunk = lax.dynamic_index_in_dim(received, jnp.clip(peer, 0, peers - 1), 0, keepdims=False)
    return jnp.where(ok, chunk, jnp.zeros_like(chunk))


def velocity_kernel(idx_ref, src_ref, main_ref, halo_ref, out_main_ref, out_halo_ref):
    total = idx_ref[idx_ref.shape[0] - 1]
    main = tuple(main_ref[k] for k in range(6))
    halo = tuple(halo_ref[k] for k in range(6))
    upper = lax.broadcasted_iota(jnp.int32, main[0].shape, 0) < main[0].shape[0] // 2

    def load(at):
        return src_ref[at], src_ref[at + SC], src_ref[at + 2 * SC], src_ref[at + 3 * SC]

    def term(targ, src, acc):
        tx, ty, tz, nx, ny, nz = targ
        sx, sy, sz, q = src
        dx = tx - sx
        dy = ty - sy
        dz = tz - sz
        dist2 = dx * dx + dy * dy + dz * dz + EPS2
        numer = nx * dx + ny * dy + nz * dz
        r = lax.rsqrt(dist2)
        return acc + (q * numer) * (r * r * r)

    def block(b, accs):
        acc_m, acc_h = accs
        first = b * BLOCK
        for u in range(0, BLOCK, 2):
            one = load(idx_ref[first + u])
            two = load(idx_ref[first + u + 1])
            acc_m = term(main, one, acc_m)
            acc_m = term(main, two, acc_m)
            both = tuple(jnp.where(upper, x, y) for x, y in zip(one, two))
            acc_h = term(halo, both, acc_h)
        return acc_m, acc_h

    blocks = (total + (BLOCK - 1)) // BLOCK
    zero = jnp.zeros(main[0].shape, jnp.float32)
    acc_m, acc_h = lax.fori_loop(0, blocks, block, (zero, zero))
    half = acc_h.shape[0] // 2
    out_main_ref[...] = acc_m
    out_halo_ref[...] = acc_h[:half] + acc_h[half:]


def live_slots(group_len, slots):
    lengths = group_len.T.reshape(-1)
    ends = jnp.cumsum(lengths)
    at = jnp.arange(slots, dtype=jnp.int32)
    passed = ends[None, :] <= at[:, None]
    segment = jnp.sum(passed.astype(jnp.int32), axis=1)
    before = jnp.sum(jnp.where(passed, lengths[None, :], 0), axis=1)
    total = ends[-1]
    idx = jnp.where(at < total, segment * (4 * SC) + (at - before), slots * 4)
    return jnp.concatenate([idx, total[None]])


def velocity(idx, src, main, halo):
    half = jax.ShapeDtypeStruct((halo.shape[1] // 2, halo.shape[2]), jnp.float32)
    return pl.pallas_call(
        velocity_kernel,
        out_shape=(jax.ShapeDtypeStruct(main.shape[1:], jnp.float32), half),
        in_specs=[
            pl.BlockSpec(memory_space=pltpu.SMEM),
            pl.BlockSpec(memory_space=pltpu.SMEM),
            pl.BlockSpec(memory_space=pltpu.VMEM),
            pl.BlockSpec(memory_space=pltpu.VMEM),
        ],
        out_specs=(pl.BlockSpec(memory_space=pltpu.VMEM), pl.BlockSpec(memory_space=pltpu.VMEM)),
    )(idx, src, main, halo)


def tendency(ext, vel):
    centre = ext[:, 1:-1, 1:-1]
    grad_x = (ext[:, 2:, 1:-1] - ext[:, :-2, 1:-1]) * 0.5
    grad_y = (ext[:, 1:-1, 2:] - ext[:, 1:-1, :-2]) * 0.5
    slope = 1.0 + grad_x[0] * grad_x[0] + grad_y[0] * grad_y[0]
    eta_rate = vel * slope - (grad_x[1] * grad_x[0] + grad_y[1] * grad_y[0])
    phi_rate = (
        -centre[0]
        - 0.5 * (grad_x[1] * grad_x[1] + grad_y[1] * grad_y[1])
        + 0.5 * vel * vel * slope
    )
    return jnp.stack([eta_rate, phi_rate])


def smooth(rim):
    centre = rim[:, 1:-1, 1:-1]
    return (
        4.0 * centre + rim[:, 2:, 1:-1] + rim[:, :-2, 1:-1] + rim[:, 1:-1, 2:] + rim[:, 1:-1, :-2]
    ) / 8.0


def body(target_geom, eta, phi, sources, group_len, owner):
    rows_here, cols_here = eta.shape
    n_tile, n_eval = lax.axis_size("tile"), lax.axis_size("eval")
    row = lax.axis_index("tile")
    column = lax.axis_index("eval")
    width = sources.shape[-1]
    group_len = group_len[:ROUNDS]
    owner = owner[:ROUNDS]

    fields = jnp.stack([eta, phi])
    own_block = sources[0].reshape(-1)
    top = jnp.concatenate([fields[:, :2].reshape(-1), target_geom[:, 0].reshape(-1)])
    bottom = jnp.concatenate([fields[:, -2:].reshape(-1), target_geom[:, -1].reshape(-1)])
    to_above = (jnp.arange(n_tile, dtype=jnp.int32) == row - 1)[:, None]
    payload = jnp.concatenate([
        jnp.broadcast_to(own_block[None], (n_tile, own_block.shape[0])),
        jnp.where(to_above, top[None], bottom[None]),
    ], axis=1)
    got = lax.all_to_all(payload, "tile", 0, 0, tiled=True)
    n_own = own_block.shape[0]
    src_rows = got[:, :n_own].reshape(n_tile, ROUNDS, n_own // ROUNDS)
    stacked = src_rows[owner, jnp.arange(ROUNDS)]
    rim = 2 * cols_here * 2
    above = from_peer(got[:, n_own:], row, -1, n_tile)
    below = from_peer(got[:, n_own:], row, 1, n_tile)
    f_above = above[:rim].reshape(2, 2, cols_here)
    f_below = below[:rim].reshape(2, 2, cols_here)
    t_above = above[rim:].reshape(6, cols_here)
    t_below = below[rim:].reshape(6, cols_here)
    ext_rows = jnp.concatenate([f_above, fields, f_below], axis=1)

    n_src = ROUNDS * 4 * width
    left_rim = jnp.concatenate([ext_rows[:, :, :2].reshape(-1), target_geom[:, :, 0].reshape(-1)])
    right_rim = jnp.concatenate([ext_rows[:, :, -2:].reshape(-1), target_geom[:, :, -1].reshape(-1)])
    to_left = (jnp.arange(n_eval, dtype=jnp.int32) == column - 1)[:, None]
    payload = jnp.concatenate([
        jnp.broadcast_to(stacked.reshape(-1)[None], (n_eval, n_src)),
        jnp.where(to_left, left_rim[None], right_rim[None]),
    ], axis=1)
    got = lax.all_to_all(payload, "eval", 0, 0, tiled=True)
    all_src = jnp.concatenate([got[:, :n_src].reshape(-1), jnp.zeros((4 * SC,), jnp.float32)])
    idx = live_slots(group_len, n_eval * ROUNDS * width)
    rim = 2 * (rows_here + 4) * 2
    left = from_peer(got[:, n_src:], column, -1, n_eval)
    right = from_peer(got[:, n_src:], column, 1, n_eval)
    f_left = left[:rim].reshape(2, rows_here + 4, 2)
    f_right = right[:rim].reshape(2, rows_here + 4, 2)
    t_left = left[rim:].reshape(6, rows_here)
    t_right = right[rim:].reshape(6, rows_here)
    ext = jnp.concatenate([f_left, ext_rows, f_right], axis=2)

    sides = jnp.concatenate([t_left, t_right], axis=1)
    sides = jnp.pad(sides, ((0, 0), (0, cols_here - 2 * rows_here)))
    halo = jnp.stack([t_above, t_below, sides, jnp.zeros_like(sides)], axis=1)
    halo = jnp.concatenate([halo, halo], axis=1)
    vel_main, vel_halo = velocity(idx, all_src, target_geom, halo)
    vel_up = vel_halo[0:1]
    vel_down = vel_halo[1:2]
    vel_left = vel_halo[2, :rows_here][:, None]
    vel_right = vel_halo[2, rows_here:2 * rows_here][:, None]

    vel_rows = jnp.concatenate([vel_up, vel_main, vel_down], axis=0)
    corner = jnp.zeros((1, 1), jnp.float32)
    vel_l = jnp.concatenate([corner, vel_left, corner], axis=0)
    vel_r = jnp.concatenate([corner, vel_right, corner], axis=0)
    vel = jnp.concatenate([vel_l, vel_rows, vel_r], axis=1)
    rates = tendency(ext, vel)
    row_ids = row * rows_here + jnp.arange(rows_here + 2, dtype=jnp.int32) - 1
    col_ids = column * cols_here + jnp.arange(cols_here + 2, dtype=jnp.int32) - 1
    row_ok = (row_ids >= 0) & (row_ids < rows_here * n_tile)
    col_ok = (col_ids >= 0) & (col_ids < cols_here * n_eval)
    inside = (row_ok[:, None] & col_ok[None, :]).astype(jnp.float32)
    smoothed = smooth(rates * inside[None])
    return (eta + 0.5 * smoothed[0], phi + 0.5 * smoothed[1], vel_main)


def solution(mesh):
    return jax.shard_map(
        body,
        mesh=mesh,
        in_specs=(
            P(None, "tile", "eval"),
            P("tile", "eval"),
            P("tile", "eval"),
            P("tile", None, None, "eval"),
            P(),
            P(),
        ),
        out_specs=(P("tile", "eval"), P("tile", "eval"), P("tile", "eval")),
        check_vma=False,
    )
```

```python
import functools

import jax
import jax.numpy as jnp
from jax import lax
from jax.experimental import pallas as pl
from jax.experimental.pallas import tpu as pltpu
from jax.sharding import PartitionSpec as P

ROUNDS = 4
SC = 32
BLOCK = 64

EPS2 = 0.05


def copy_for_each(x, axis):
    peers = lax.axis_size(axis)
    return lax.all_to_all(jnp.broadcast_to(x[None], (peers, *x.shape)), axis, 0, 0, tiled=True)


def from_peer(received, me, offset, peers):
    peer = me + offset
    ok = (peer >= 0) & (peer < peers)
    chunk = lax.dynamic_index_in_dim(received, jnp.clip(peer, 0, peers - 1), 0, keepdims=False)
    return jnp.where(ok, chunk, jnp.zeros_like(chunk))


def velocity_kernel(idx_ref, src_ref, main_ref, halo_ref, out_main_ref, out_up_ref, out_down_ref, out_side_ref):
    total = idx_ref[idx_ref.shape[0] - 1]
    main = tuple(main_ref[k] for k in range(6))
    halo = tuple(halo_ref[k] for k in range(6))
    upper = lax.broadcasted_iota(jnp.int32, main[0].shape, 0) < main[0].shape[0] // 2

    def load(at):
        return src_ref[at], src_ref[at + SC], src_ref[at + 2 * SC], src_ref[at + 3 * SC]

    def term(targ, src, acc):
        tx, ty, tz, nx, ny, nz = targ
        sx, sy, sz, q = src
        dx = tx - sx
        dy = ty - sy
        dz = tz - sz
        dist2 = dx * dx + dy * dy + dz * dz + EPS2
        numer = nx * dx + ny * dy + nz * dz
        r = lax.rsqrt(dist2)
        return acc + (q * numer) * (r * r * r)

    def block(b, accs):
        acc_m, acc_h = accs
        first = b * BLOCK
        for u in range(0, BLOCK, 2):
            one = load(idx_ref[first + u])
            two = load(idx_ref[first + u + 1])
            acc_m = term(main, one, acc_m)
            acc_m = term(main, two, acc_m)
            both = tuple(jnp.where(upper, x, y) for x, y in zip(one, two))
            acc_h = term(halo, both, acc_h)
        return acc_m, acc_h

    blocks = (total + (BLOCK - 1)) // BLOCK
    zero = jnp.zeros(main[0].shape, jnp.float32)
    acc_m, acc_h = lax.fori_loop(0, blocks, block, (zero, zero))
    half = acc_h.shape[0] // 2
    out_main_ref[...] = acc_m
    acc_h = acc_h[:half] + acc_h[half:]
    out_up_ref[...] = acc_h[0:1]
    out_down_ref[...] = acc_h[1:2]
    out_side_ref[...] = acc_h[2:3]


def live_slots(group_len, slots):
    lengths = group_len.T.reshape(-1)
    ends = jnp.cumsum(lengths)
    at = jnp.arange(slots, dtype=jnp.int32)
    passed = ends[None, :] <= at[:, None]
    segment = jnp.sum(passed.astype(jnp.int32), axis=1)
    before = jnp.sum(jnp.where(passed, lengths[None, :], 0), axis=1)
    total = ends[-1]
    idx = jnp.where(at < total, segment * (4 * SC) + (at - before), slots * 4)
    return jnp.concatenate([idx, total[None]])


def velocity(idx, src, main, halo):
    row = jax.ShapeDtypeStruct((1, halo.shape[2]), jnp.float32)
    return pl.pallas_call(
        velocity_kernel,
        out_shape=(jax.ShapeDtypeStruct(main.shape[1:], jnp.float32), row, row, row),
        in_specs=[
            pl.BlockSpec(memory_space=pltpu.SMEM),
            pl.BlockSpec(memory_space=pltpu.SMEM),
            pl.BlockSpec(memory_space=pltpu.VMEM),
            pl.BlockSpec(memory_space=pltpu.VMEM),
        ],
        out_specs=tuple(pl.BlockSpec(memory_space=pltpu.VMEM) for _ in range(4)),
    )(idx, src, main, halo)


def tendency(ext, vel):
    centre = ext[:, 1:-1, 1:-1]
    grad_x = (ext[:, 2:, 1:-1] - ext[:, :-2, 1:-1]) * 0.5
    grad_y = (ext[:, 1:-1, 2:] - ext[:, 1:-1, :-2]) * 0.5
    slope = 1.0 + grad_x[0] * grad_x[0] + grad_y[0] * grad_y[0]
    eta_rate = vel * slope - (grad_x[1] * grad_x[0] + grad_y[1] * grad_y[0])
    phi_rate = (
        -centre[0]
        - 0.5 * (grad_x[1] * grad_x[1] + grad_y[1] * grad_y[1])
        + 0.5 * vel * vel * slope
    )
    return jnp.stack([eta_rate, phi_rate])


def smooth(rim):
    centre = rim[:, 1:-1, 1:-1]
    return (
        4.0 * centre + rim[:, 2:, 1:-1] + rim[:, :-2, 1:-1] + rim[:, 1:-1, 2:] + rim[:, 1:-1, :-2]
    ) / 8.0


def body(target_geom, eta, phi, sources, group_len, owner):
    rows_here, cols_here = eta.shape
    n_tile, n_eval = lax.axis_size("tile"), lax.axis_size("eval")
    row = lax.axis_index("tile")
    column = lax.axis_index("eval")
    width = sources.shape[-1]
    group_len = group_len[:ROUNDS]
    owner = owner[:ROUNDS]

    fields = jnp.stack([eta, phi])
    mine = (owner == row).astype(jnp.float32)
    own_block = jnp.sum(mine[:, None, None] * sources[0], axis=0).reshape(-1)
    top = jnp.concatenate([fields[:, :2].reshape(-1), target_geom[:, 0].reshape(-1)])
    bottom = jnp.concatenate([fields[:, -2:].reshape(-1), target_geom[:, -1].reshape(-1)])
    to_above = (jnp.arange(n_tile, dtype=jnp.int32) == row - 1)[:, None]
    payload = jnp.concatenate([
        jnp.broadcast_to(own_block[None], (n_tile, own_block.shape[0])),
        jnp.where(to_above, top[None], bottom[None]),
    ], axis=1)
    got = lax.all_to_all(payload, "tile", 0, 0, tiled=True)
    n_own = own_block.shape[0]
    stacked = got[:, :n_own][owner]
    rim = 2 * cols_here * 2
    above = from_peer(got[:, n_own:], row, -1, n_tile)
    below = from_peer(got[:, n_own:], row, 1, n_tile)
    f_above = above[:rim].reshape(2, 2, cols_here)
    f_below = below[:rim].reshape(2, 2, cols_here)
    t_above = above[rim:].reshape(6, cols_here)
    t_below = below[rim:].reshape(6, cols_here)
    ext_rows = jnp.concatenate([f_above, fields, f_below], axis=1)

    n_src = ROUNDS * 4 * width
    left_rim = jnp.concatenate([ext_rows[:, :, :2].reshape(-1), target_geom[:, :, 0].reshape(-1)])
    right_rim = jnp.concatenate([ext_rows[:, :, -2:].reshape(-1), target_geom[:, :, -1].reshape(-1)])
    to_left = (jnp.arange(n_eval, dtype=jnp.int32) == column - 1)[:, None]
    payload = jnp.concatenate([
        jnp.broadcast_to(stacked.reshape(-1)[None], (n_eval, n_src)),
        jnp.where(to_left, left_rim[None], right_rim[None]),
    ], axis=1)
    got = lax.all_to_all(payload, "eval", 0, 0, tiled=True)
    all_src = jnp.concatenate([got[:, :n_src].reshape(-1), jnp.zeros((4 * SC,), jnp.float32)])
    idx = live_slots(group_len, n_eval * ROUNDS * width)
    rim = 2 * (rows_here + 4) * 2
    left = from_peer(got[:, n_src:], column, -1, n_eval)
    right = from_peer(got[:, n_src:], column, 1, n_eval)
    f_left = left[:rim].reshape(2, rows_here + 4, 2)
    f_right = right[:rim].reshape(2, rows_here + 4, 2)
    t_left = left[rim:].reshape(6, rows_here)
    t_right = right[rim:].reshape(6, rows_here)
    ext = jnp.concatenate([f_left, ext_rows, f_right], axis=2)

    sides = jnp.concatenate([t_left, t_right], axis=1)
    sides = jnp.pad(sides, ((0, 0), (0, cols_here - 2 * rows_here)))
    halo = jnp.stack([t_above, t_below, sides, jnp.zeros_like(sides)], axis=1)
    halo = jnp.concatenate([halo, halo], axis=1)
    vel_main, vel_up, vel_down, vel_side = velocity(idx, all_src, target_geom, halo)
    vel_left = vel_side[0, :rows_here][:, None]
    vel_right = vel_side[0, rows_here:2 * rows_here][:, None]

    vel_rows = jnp.concatenate([vel_up, vel_main, vel_down], axis=0)
    corner = jnp.zeros((1, 1), jnp.float32)
    vel_l = jnp.concatenate([corner, vel_left, corner], axis=0)
    vel_r = jnp.concatenate([corner, vel_right, corner], axis=0)
    vel = jnp.concatenate([vel_l, vel_rows, vel_r], axis=1)
    rates = tendency(ext, vel)
    row_ids = row * rows_here + jnp.arange(rows_here + 2, dtype=jnp.int32) - 1
    col_ids = column * cols_here + jnp.arange(cols_here + 2, dtype=jnp.int32) - 1
    row_ok = (row_ids >= 0) & (row_ids < rows_here * n_tile)
    col_ok = (col_ids >= 0) & (col_ids < cols_here * n_eval)
    inside = (row_ok[:, None] & col_ok[None, :]).astype(jnp.float32)
    smoothed = smooth(rates * inside[None])
    return (eta + 0.5 * smoothed[0], phi + 0.5 * smoothed[1], vel_main)


def solution(mesh):
    return jax.shard_map(
        body,
        mesh=mesh,
        in_specs=(
            P(None, "tile", "eval"),
            P("tile", "eval"),
            P("tile", "eval"),
            P("tile", None, None, "eval"),
            P(),
            P(),
        ),
        out_specs=(P("tile", "eval"), P("tile", "eval"), P("tile", "eval")),
        check_vma=False,
    )
```

```python
import functools

import jax
import jax.numpy as jnp
from jax import lax
from jax.experimental import pallas as pl
from jax.experimental.pallas import tpu as pltpu
from jax.sharding import PartitionSpec as P

ROUNDS = 4
SC = 32
BLOCK = 64

EPS2 = 0.05


def copy_for_each(x, axis):
    peers = lax.axis_size(axis)
    return lax.all_to_all(jnp.broadcast_to(x[None], (peers, *x.shape)), axis, 0, 0, tiled=True)


def from_peer(received, me, offset, peers):
    peer = me + offset
    ok = (peer >= 0) & (peer < peers)
    chunk = lax.dynamic_index_in_dim(received, jnp.clip(peer, 0, peers - 1), 0, keepdims=False)
    return jnp.where(ok, chunk, jnp.zeros_like(chunk))


def velocity_kernel(idx_ref, src_ref, main_ref, halo_ref, out_main_ref, out_up_ref, out_down_ref, out_left_ref, out_right_ref):
    total = idx_ref[idx_ref.shape[0] - 1]
    main = tuple(main_ref[k] for k in range(6))
    halo = tuple(halo_ref[k] for k in range(6))
    upper = lax.broadcasted_iota(jnp.int32, main[0].shape, 0) < main[0].shape[0] // 2

    def load(at):
        return src_ref[at], src_ref[at + SC], src_ref[at + 2 * SC], src_ref[at + 3 * SC]

    def term(targ, src, acc):
        tx, ty, tz, nx, ny, nz = targ
        sx, sy, sz, q = src
        dx = tx - sx
        dy = ty - sy
        dz = tz - sz
        dist2 = dx * dx + dy * dy + dz * dz + EPS2
        numer = nx * dx + ny * dy + nz * dz
        r = lax.rsqrt(dist2)
        return acc + (q * numer) * (r * r * r)

    def block(b, accs):
        acc_m, acc_h = accs
        first = b * BLOCK
        for u in range(0, BLOCK, 2):
            one = load(idx_ref[first + u])
            two = load(idx_ref[first + u + 1])
            acc_m = term(main, one, acc_m)
            acc_m = term(main, two, acc_m)
            both = tuple(jnp.where(upper, x, y) for x, y in zip(one, two))
            acc_h = term(halo, both, acc_h)
        return acc_m, acc_h

    blocks = (total + (BLOCK - 1)) // BLOCK
    zero = jnp.zeros(main[0].shape, jnp.float32)
    acc_m, acc_h = lax.fori_loop(0, blocks, block, (zero, zero))
    half = acc_h.shape[0] // 2
    out_main_ref[...] = acc_m
    acc_h = acc_h[:half] + acc_h[half:]
    out_up_ref[...] = acc_h[0:1]
    out_down_ref[...] = acc_h[1:2]
    rows = out_left_ref.shape[0]
    columns = jnp.transpose(jnp.concatenate([acc_h, acc_h]))
    out_left_ref[...] = columns[0:rows, 2:3]
    out_right_ref[...] = columns[rows:2 * rows, 2:3]


def live_slots(group_len, slots):
    lengths = group_len.T.reshape(-1)
    ends = jnp.cumsum(lengths)
    at = jnp.arange(slots, dtype=jnp.int32)
    passed = ends[None, :] <= at[:, None]
    segment = jnp.sum(passed.astype(jnp.int32), axis=1)
    before = jnp.sum(jnp.where(passed, lengths[None, :], 0), axis=1)
    total = ends[-1]
    idx = jnp.where(at < total, segment * (4 * SC) + (at - before), slots * 4)
    return jnp.concatenate([idx, total[None]])


def velocity(idx, src, main, halo):
    row = jax.ShapeDtypeStruct((1, halo.shape[2]), jnp.float32)
    column = jax.ShapeDtypeStruct((main.shape[1], 1), jnp.float32)
    return pl.pallas_call(
        velocity_kernel,
        out_shape=(jax.ShapeDtypeStruct(main.shape[1:], jnp.float32), row, row, column, column),
        in_specs=[
            pl.BlockSpec(memory_space=pltpu.SMEM),
            pl.BlockSpec(memory_space=pltpu.SMEM),
            pl.BlockSpec(memory_space=pltpu.VMEM),
            pl.BlockSpec(memory_space=pltpu.VMEM),
        ],
        out_specs=tuple(pl.BlockSpec(memory_space=pltpu.VMEM) for _ in range(5)),
    )(idx, src, main, halo)


def tendency(ext, vel):
    centre = ext[:, 1:-1, 1:-1]
    grad_x = (ext[:, 2:, 1:-1] - ext[:, :-2, 1:-1]) * 0.5
    grad_y = (ext[:, 1:-1, 2:] - ext[:, 1:-1, :-2]) * 0.5
    slope = 1.0 + grad_x[0] * grad_x[0] + grad_y[0] * grad_y[0]
    eta_rate = vel * slope - (grad_x[1] * grad_x[0] + grad_y[1] * grad_y[0])
    phi_rate = (
        -centre[0]
        - 0.5 * (grad_x[1] * grad_x[1] + grad_y[1] * grad_y[1])
        + 0.5 * vel * vel * slope
    )
    return jnp.stack([eta_rate, phi_rate])


def smooth(rim):
    centre = rim[:, 1:-1, 1:-1]
    return (
        4.0 * centre + rim[:, 2:, 1:-1] + rim[:, :-2, 1:-1] + rim[:, 1:-1, 2:] + rim[:, 1:-1, :-2]
    ) / 8.0


def body(target_geom, eta, phi, sources, group_len, owner):
    rows_here, cols_here = eta.shape
    n_tile, n_eval = lax.axis_size("tile"), lax.axis_size("eval")
    row = lax.axis_index("tile")
    column = lax.axis_index("eval")
    width = sources.shape[-1]
    group_len = group_len[:ROUNDS]
    owner = owner[:ROUNDS]

    fields = jnp.stack([eta, phi])
    mine = (owner == row).astype(jnp.float32)
    own_block = jnp.sum(mine[:, None, None] * sources[0], axis=0).reshape(-1)
    top = jnp.concatenate([fields[:, :2].reshape(-1), target_geom[:, 0].reshape(-1)])
    bottom = jnp.concatenate([fields[:, -2:].reshape(-1), target_geom[:, -1].reshape(-1)])
    to_above = (jnp.arange(n_tile, dtype=jnp.int32) == row - 1)[:, None]
    payload = jnp.concatenate([
        jnp.broadcast_to(own_block[None], (n_tile, own_block.shape[0])),
        jnp.where(to_above, top[None], bottom[None]),
    ], axis=1)
    got = lax.all_to_all(payload, "tile", 0, 0, tiled=True)
    n_own = own_block.shape[0]
    stacked = got[:, :n_own][owner]
    rim = 2 * cols_here * 2
    above = from_peer(got[:, n_own:], row, -1, n_tile)
    below = from_peer(got[:, n_own:], row, 1, n_tile)
    f_above = above[:rim].reshape(2, 2, cols_here)
    f_below = below[:rim].reshape(2, 2, cols_here)
    t_above = above[rim:].reshape(6, cols_here)
    t_below = below[rim:].reshape(6, cols_here)
    ext_rows = jnp.concatenate([f_above, fields, f_below], axis=1)

    n_src = ROUNDS * 4 * width
    left_rim = jnp.concatenate([ext_rows[:, :, :2].reshape(-1), target_geom[:, :, 0].reshape(-1)])
    right_rim = jnp.concatenate([ext_rows[:, :, -2:].reshape(-1), target_geom[:, :, -1].reshape(-1)])
    to_left = (jnp.arange(n_eval, dtype=jnp.int32) == column - 1)[:, None]
    payload = jnp.concatenate([
        jnp.broadcast_to(stacked.reshape(-1)[None], (n_eval, n_src)),
        jnp.where(to_left, left_rim[None], right_rim[None]),
    ], axis=1)
    got = lax.all_to_all(payload, "eval", 0, 0, tiled=True)
    all_src = jnp.concatenate([got[:, :n_src].reshape(-1), jnp.zeros((4 * SC,), jnp.float32)])
    idx = live_slots(group_len, n_eval * ROUNDS * width)
    rim = 2 * (rows_here + 4) * 2
    left = from_peer(got[:, n_src:], column, -1, n_eval)
    right = from_peer(got[:, n_src:], column, 1, n_eval)
    f_left = left[:rim].reshape(2, rows_here + 4, 2)
    f_right = right[:rim].reshape(2, rows_here + 4, 2)
    t_left = left[rim:].reshape(6, rows_here)
    t_right = right[rim:].reshape(6, rows_here)
    ext = jnp.concatenate([f_left, ext_rows, f_right], axis=2)

    sides = jnp.concatenate([t_left, t_right], axis=1)
    sides = jnp.pad(sides, ((0, 0), (0, cols_here - 2 * rows_here)))
    halo = jnp.stack([t_above, t_below, sides, jnp.zeros_like(sides)], axis=1)
    halo = jnp.concatenate([halo, halo], axis=1)
    vel_main, vel_up, vel_down, vel_left, vel_right = velocity(idx, all_src, target_geom, halo)

    vel_rows = jnp.concatenate([vel_up, vel_main, vel_down], axis=0)
    corner = jnp.zeros((1, 1), jnp.float32)
    vel_l = jnp.concatenate([corner, vel_left, corner], axis=0)
    vel_r = jnp.concatenate([corner, vel_right, corner], axis=0)
    vel = jnp.concatenate([vel_l, vel_rows, vel_r], axis=1)
    rates = tendency(ext, vel)
    row_ids = row * rows_here + jnp.arange(rows_here + 2, dtype=jnp.int32) - 1
    col_ids = column * cols_here + jnp.arange(cols_here + 2, dtype=jnp.int32) - 1
    row_ok = (row_ids >= 0) & (row_ids < rows_here * n_tile)
    col_ok = (col_ids >= 0) & (col_ids < cols_here * n_eval)
    inside = (row_ok[:, None] & col_ok[None, :]).astype(jnp.float32)
    smoothed = smooth(rates * inside[None])
    return (eta + 0.5 * smoothed[0], phi + 0.5 * smoothed[1], vel_main)


def solution(mesh):
    return jax.shard_map(
        body,
        mesh=mesh,
        in_specs=(
            P(None, "tile", "eval"),
            P("tile", "eval"),
            P("tile", "eval"),
            P("tile", None, None, "eval"),
            P(),
            P(),
        ),
        out_specs=(P("tile", "eval"), P("tile", "eval"), P("tile", "eval")),
        check_vma=False,
    )
```

```python
import functools

import jax
import jax.numpy as jnp
from jax import lax
from jax.experimental import pallas as pl
from jax.experimental.pallas import tpu as pltpu
from jax.sharding import PartitionSpec as P

ROUNDS = 4
SC = 32
BLOCK = 64

EPS2 = 0.05


def copy_for_each(x, axis):
    peers = lax.axis_size(axis)
    return lax.all_to_all(jnp.broadcast_to(x[None], (peers, *x.shape)), axis, 0, 0, tiled=True)


def from_peer(received, me, offset, peers):
    peer = me + offset
    ok = (peer >= 0) & (peer < peers)
    chunk = lax.dynamic_index_in_dim(received, jnp.clip(peer, 0, peers - 1), 0, keepdims=False)
    return jnp.where(ok, chunk, jnp.zeros_like(chunk))


def velocity_kernel(idx_ref, src_ref, main_ref, halo_ref, out_main_ref, out_up_ref, out_down_ref, out_side_ref):
    total = idx_ref[idx_ref.shape[0] - 1]
    main = tuple(main_ref[k] for k in range(6))
    halo = tuple(halo_ref[k] for k in range(6))
    upper = lax.broadcasted_iota(jnp.int32, main[0].shape, 0) < main[0].shape[0] // 2

    def load(at):
        return src_ref[at], src_ref[at + SC], src_ref[at + 2 * SC], src_ref[at + 3 * SC]

    def term(targ, src, acc):
        tx, ty, tz, nx, ny, nz = targ
        sx, sy, sz, q = src
        dx = tx - sx
        dy = ty - sy
        dz = tz - sz
        dist2 = dx * dx + dy * dy + dz * dz + EPS2
        numer = nx * dx + ny * dy + nz * dz
        r = lax.rsqrt(dist2)
        return acc + (q * numer) * (r * r * r)

    def block(b, accs):
        acc_m, acc_h = accs
        first = b * BLOCK
        for u in range(0, BLOCK, 2):
            one = load(idx_ref[first + u])
            two = load(idx_ref[first + u + 1])
            acc_m = term(main, one, acc_m)
            acc_m = term(main, two, acc_m)
            both = tuple(jnp.where(upper, x, y) for x, y in zip(one, two))
            acc_h = term(halo, both, acc_h)
        return acc_m, acc_h

    blocks = (total + (BLOCK - 1)) // BLOCK
    zero = jnp.zeros(main[0].shape, jnp.float32)
    acc_m, acc_h = lax.fori_loop(0, blocks, block, (zero, zero))
    half = acc_h.shape[0] // 2
    out_main_ref[...] = acc_m
    acc_h = acc_h[:half] + acc_h[half:]
    out_up_ref[...] = acc_h[0:1]
    out_down_ref[...] = acc_h[1:2]
    out_side_ref[...] = acc_h[2:3]


def live_slots(group_len, slots):
    lengths = group_len.T.reshape(-1)
    ends = jnp.cumsum(lengths)
    at = jnp.arange(slots, dtype=jnp.int32)
    passed = ends[None, :] <= at[:, None]
    segment = jnp.sum(passed.astype(jnp.int32), axis=1)
    before = jnp.sum(jnp.where(passed, lengths[None, :], 0), axis=1)
    total = ends[-1]
    idx = jnp.where(at < total, segment * (4 * SC) + (at - before), slots * 4)
    return jnp.concatenate([idx, total[None]])


def velocity(idx, src, main, halo):
    row = jax.ShapeDtypeStruct((1, halo.shape[2]), jnp.float32)
    return pl.pallas_call(
        velocity_kernel,
        out_shape=(jax.ShapeDtypeStruct(main.shape[1:], jnp.float32), row, row, row),
        in_specs=[
            pl.BlockSpec(memory_space=pltpu.SMEM),
            pl.BlockSpec(memory_space=pltpu.SMEM),
            pl.BlockSpec(memory_space=pltpu.VMEM),
            pl.BlockSpec(memory_space=pltpu.VMEM),
        ],
        out_specs=tuple(pl.BlockSpec(memory_space=pltpu.VMEM) for _ in range(4)),
    )(idx, src, main, halo)


def tendency(ext, vel):
    centre = ext[:, 1:-1, 1:-1]
    grad_x = (ext[:, 2:, 1:-1] - ext[:, :-2, 1:-1]) * 0.5
    grad_y = (ext[:, 1:-1, 2:] - ext[:, 1:-1, :-2]) * 0.5
    slope = 1.0 + grad_x[0] * grad_x[0] + grad_y[0] * grad_y[0]
    eta_rate = vel * slope - (grad_x[1] * grad_x[0] + grad_y[1] * grad_y[0])
    phi_rate = (
        -centre[0]
        - 0.5 * (grad_x[1] * grad_x[1] + grad_y[1] * grad_y[1])
        + 0.5 * vel * vel * slope
    )
    return jnp.stack([eta_rate, phi_rate])


def smooth(rim):
    centre = rim[:, 1:-1, 1:-1]
    return (
        4.0 * centre + rim[:, 2:, 1:-1] + rim[:, :-2, 1:-1] + rim[:, 1:-1, 2:] + rim[:, 1:-1, :-2]
    ) / 8.0


def body(target_geom, eta, phi, sources, group_len, owner):
    rows_here, cols_here = eta.shape
    n_tile, n_eval = lax.axis_size("tile"), lax.axis_size("eval")
    row = lax.axis_index("tile")
    column = lax.axis_index("eval")
    width = sources.shape[-1]
    group_len = group_len[:ROUNDS]
    owner = owner[:ROUNDS]

    fields = jnp.stack([eta, phi])
    own_block = sources[0].reshape(-1)
    top = jnp.concatenate([fields[:, :2].reshape(-1), target_geom[:, 0].reshape(-1)])
    bottom = jnp.concatenate([fields[:, -2:].reshape(-1), target_geom[:, -1].reshape(-1)])
    to_above = (jnp.arange(n_tile, dtype=jnp.int32) == row - 1)[:, None]
    payload = jnp.concatenate([
        jnp.broadcast_to(own_block[None], (n_tile, own_block.shape[0])),
        jnp.where(to_above, top[None], bottom[None]),
    ], axis=1)
    got = lax.all_to_all(payload, "tile", 0, 0, tiled=True)
    n_own = own_block.shape[0]
    src_rows = got[:, :n_own].reshape(n_tile, ROUNDS, n_own // ROUNDS)
    stacked = src_rows[owner, jnp.arange(ROUNDS)]
    rim = 2 * cols_here * 2
    above = from_peer(got[:, n_own:], row, -1, n_tile)
    below = from_peer(got[:, n_own:], row, 1, n_tile)
    f_above = above[:rim].reshape(2, 2, cols_here)
    f_below = below[:rim].reshape(2, 2, cols_here)
    t_above = above[rim:].reshape(6, cols_here)
    t_below = below[rim:].reshape(6, cols_here)
    ext_rows = jnp.concatenate([f_above, fields, f_below], axis=1)

    n_src = ROUNDS * 4 * width
    left_rim = jnp.concatenate([ext_rows[:, :, :2].reshape(-1), target_geom[:, :, 0].reshape(-1)])
    right_rim = jnp.concatenate([ext_rows[:, :, -2:].reshape(-1), target_geom[:, :, -1].reshape(-1)])
    to_left = (jnp.arange(n_eval, dtype=jnp.int32) == column - 1)[:, None]
    payload = jnp.concatenate([
        jnp.broadcast_to(stacked.reshape(-1)[None], (n_eval, n_src)),
        jnp.where(to_left, left_rim[None], right_rim[None]),
    ], axis=1)
    got = lax.all_to_all(payload, "eval", 0, 0, tiled=True)
    all_src = jnp.concatenate([got[:, :n_src].reshape(-1), jnp.zeros((4 * SC,), jnp.float32)])
    idx = live_slots(group_len, n_eval * ROUNDS * width)
    rim = 2 * (rows_here + 4) * 2
    left = from_peer(got[:, n_src:], column, -1, n_eval)
    right = from_peer(got[:, n_src:], column, 1, n_eval)
    f_left = left[:rim].reshape(2, rows_here + 4, 2)
    f_right = right[:rim].reshape(2, rows_here + 4, 2)
    t_left = left[rim:].reshape(6, rows_here)
    t_right = right[rim:].reshape(6, rows_here)
    ext = jnp.concatenate([f_left, ext_rows, f_right], axis=2)

    sides = jnp.concatenate([t_left, t_right], axis=1)
    sides = jnp.pad(sides, ((0, 0), (0, cols_here - 2 * rows_here)))
    halo = jnp.stack([t_above, t_below, sides, jnp.zeros_like(sides)], axis=1)
    halo = jnp.concatenate([halo, halo], axis=1)
    vel_main, vel_up, vel_down, vel_side = velocity(idx, all_src, target_geom, halo)
    vel_left = vel_side[0, :rows_here][:, None]
    vel_right = vel_side[0, rows_here:2 * rows_here][:, None]

    vel_rows = jnp.concatenate([vel_up, vel_main, vel_down], axis=0)
    corner = jnp.zeros((1, 1), jnp.float32)
    vel_l = jnp.concatenate([corner, vel_left, corner], axis=0)
    vel_r = jnp.concatenate([corner, vel_right, corner], axis=0)
    vel = jnp.concatenate([vel_l, vel_rows, vel_r], axis=1)
    rates = tendency(ext, vel)
    row_ids = row * rows_here + jnp.arange(rows_here + 2, dtype=jnp.int32) - 1
    col_ids = column * cols_here + jnp.arange(cols_here + 2, dtype=jnp.int32) - 1
    row_ok = (row_ids >= 0) & (row_ids < rows_here * n_tile)
    col_ok = (col_ids >= 0) & (col_ids < cols_here * n_eval)
    inside = (row_ok[:, None] & col_ok[None, :]).astype(jnp.float32)
    smoothed = smooth(rates * inside[None])
    return (eta + 0.5 * smoothed[0], phi + 0.5 * smoothed[1], vel_main)


def solution(mesh):
    return jax.shard_map(
        body,
        mesh=mesh,
        in_specs=(
            P(None, "tile", "eval"),
            P("tile", "eval"),
            P("tile", "eval"),
            P("tile", None, None, "eval"),
            P(),
            P(),
        ),
        out_specs=(P("tile", "eval"), P("tile", "eval"), P("tile", "eval")),
        check_vma=False,
    )
```

```python
import functools

import jax
import jax.numpy as jnp
from jax import lax
from jax.experimental import pallas as pl
from jax.experimental.pallas import tpu as pltpu
from jax.sharding import PartitionSpec as P

ROUNDS = 4
SC = 32
BLOCK = 128

EPS2 = 0.05


def copy_for_each(x, axis):
    peers = lax.axis_size(axis)
    return lax.all_to_all(jnp.broadcast_to(x[None], (peers, *x.shape)), axis, 0, 0, tiled=True)


def from_peer(received, me, offset, peers):
    peer = me + offset
    ok = (peer >= 0) & (peer < peers)
    chunk = lax.dynamic_index_in_dim(received, jnp.clip(peer, 0, peers - 1), 0, keepdims=False)
    return jnp.where(ok, chunk, jnp.zeros_like(chunk))


def velocity_kernel(idx_ref, src_ref, main_ref, halo_ref, out_main_ref, out_up_ref, out_down_ref, out_side_ref):
    total = idx_ref[idx_ref.shape[0] - 1]
    main = tuple(main_ref[k] for k in range(6))
    halo = tuple(halo_ref[k] for k in range(6))
    upper = lax.broadcasted_iota(jnp.int32, main[0].shape, 0) < main[0].shape[0] // 2

    def load(at):
        return src_ref[at], src_ref[at + SC], src_ref[at + 2 * SC], src_ref[at + 3 * SC]

    def term(targ, src, acc):
        tx, ty, tz, nx, ny, nz = targ
        sx, sy, sz, q = src
        dx = tx - sx
        dy = ty - sy
        dz = tz - sz
        dist2 = dx * dx + dy * dy + dz * dz + EPS2
        numer = nx * dx + ny * dy + nz * dz
        r = lax.rsqrt(dist2)
        return acc + (q * numer) * (r * r * r)

    def block(b, accs):
        acc_m, acc_h = accs
        first = b * BLOCK
        for u in range(0, BLOCK, 2):
            one = load(idx_ref[first + u])
            two = load(idx_ref[first + u + 1])
            acc_m = term(main, one, acc_m)
            acc_m = term(main, two, acc_m)
            both = tuple(jnp.where(upper, x, y) for x, y in zip(one, two))
            acc_h = term(halo, both, acc_h)
        return acc_m, acc_h

    blocks = (total + (BLOCK - 1)) // BLOCK
    zero = jnp.zeros(main[0].shape, jnp.float32)
    acc_m, acc_h = lax.fori_loop(0, blocks, block, (zero, zero))
    half = acc_h.shape[0] // 2
    out_main_ref[...] = acc_m
    acc_h = acc_h[:half] + acc_h[half:]
    out_up_ref[...] = acc_h[0:1]
    out_down_ref[...] = acc_h[1:2]
    out_side_ref[...] = acc_h[2:3]


def live_slots(group_len, slots):
    lengths = group_len.T.reshape(-1)
    ends = jnp.cumsum(lengths)
    at = jnp.arange(slots, dtype=jnp.int32)
    passed = ends[None, :] <= at[:, None]
    segment = jnp.sum(passed.astype(jnp.int32), axis=1)
    before = jnp.sum(jnp.where(passed, lengths[None, :], 0), axis=1)
    total = ends[-1]
    idx = jnp.where(at < total, segment * (4 * SC) + (at - before), slots * 4)
    return jnp.concatenate([idx, total[None]])


def velocity(idx, src, main, halo):
    row = jax.ShapeDtypeStruct((1, halo.shape[2]), jnp.float32)
    return pl.pallas_call(
        velocity_kernel,
        out_shape=(jax.ShapeDtypeStruct(main.shape[1:], jnp.float32), row, row, row),
        in_specs=[
            pl.BlockSpec(memory_space=pltpu.SMEM),
            pl.BlockSpec(memory_space=pltpu.SMEM),
            pl.BlockSpec(memory_space=pltpu.VMEM),
            pl.BlockSpec(memory_space=pltpu.VMEM),
        ],
        out_specs=tuple(pl.BlockSpec(memory_space=pltpu.VMEM) for _ in range(4)),
    )(idx, src, main, halo)


def tendency(ext, vel):
    centre = ext[:, 1:-1, 1:-1]
    grad_x = (ext[:, 2:, 1:-1] - ext[:, :-2, 1:-1]) * 0.5
    grad_y = (ext[:, 1:-1, 2:] - ext[:, 1:-1, :-2]) * 0.5
    slope = 1.0 + grad_x[0] * grad_x[0] + grad_y[0] * grad_y[0]
    eta_rate = vel * slope - (grad_x[1] * grad_x[0] + grad_y[1] * grad_y[0])
    phi_rate = (
        -centre[0]
        - 0.5 * (grad_x[1] * grad_x[1] + grad_y[1] * grad_y[1])
        + 0.5 * vel * vel * slope
    )
    return jnp.stack([eta_rate, phi_rate])


def smooth(rim):
    centre = rim[:, 1:-1, 1:-1]
    return (
        4.0 * centre + rim[:, 2:, 1:-1] + rim[:, :-2, 1:-1] + rim[:, 1:-1, 2:] + rim[:, 1:-1, :-2]
    ) / 8.0


def body(target_geom, eta, phi, sources, group_len, owner):
    rows_here, cols_here = eta.shape
    n_tile, n_eval = lax.axis_size("tile"), lax.axis_size("eval")
    row = lax.axis_index("tile")
    column = lax.axis_index("eval")
    width = sources.shape[-1]
    group_len = group_len[:ROUNDS]
    owner = owner[:ROUNDS]

    fields = jnp.stack([eta, phi])
    mine = (owner == row).astype(jnp.float32)
    own_block = jnp.sum(mine[:, None, None] * sources[0], axis=0).reshape(-1)
    top = jnp.concatenate([fields[:, :2].reshape(-1), target_geom[:, 0].reshape(-1)])
    bottom = jnp.concatenate([fields[:, -2:].reshape(-1), target_geom[:, -1].reshape(-1)])
    to_above = (jnp.arange(n_tile, dtype=jnp.int32) == row - 1)[:, None]
    payload = jnp.concatenate([
        jnp.broadcast_to(own_block[None], (n_tile, own_block.shape[0])),
        jnp.where(to_above, top[None], bottom[None]),
    ], axis=1)
    got = lax.all_to_all(payload, "tile", 0, 0, tiled=True)
    n_own = own_block.shape[0]
    stacked = got[:, :n_own][owner]
    rim = 2 * cols_here * 2
    above = from_peer(got[:, n_own:], row, -1, n_tile)
    below = from_peer(got[:, n_own:], row, 1, n_tile)
    f_above = above[:rim].reshape(2, 2, cols_here)
    f_below = below[:rim].reshape(2, 2, cols_here)
    t_above = above[rim:].reshape(6, cols_here)
    t_below = below[rim:].reshape(6, cols_here)
    ext_rows = jnp.concatenate([f_above, fields, f_below], axis=1)

    n_src = ROUNDS * 4 * width
    left_rim = jnp.concatenate([ext_rows[:, :, :2].reshape(-1), target_geom[:, :, 0].reshape(-1)])
    right_rim = jnp.concatenate([ext_rows[:, :, -2:].reshape(-1), target_geom[:, :, -1].reshape(-1)])
    to_left = (jnp.arange(n_eval, dtype=jnp.int32) == column - 1)[:, None]
    payload = jnp.concatenate([
        jnp.broadcast_to(stacked.reshape(-1)[None], (n_eval, n_src)),
        jnp.where(to_left, left_rim[None], right_rim[None]),
    ], axis=1)
    got = lax.all_to_all(payload, "eval", 0, 0, tiled=True)
    all_src = jnp.concatenate([got[:, :n_src].reshape(-1), jnp.zeros((4 * SC,), jnp.float32)])
    idx = live_slots(group_len, n_eval * ROUNDS * width)
    rim = 2 * (rows_here + 4) * 2
    left = from_peer(got[:, n_src:], column, -1, n_eval)
    right = from_peer(got[:, n_src:], column, 1, n_eval)
    f_left = left[:rim].reshape(2, rows_here + 4, 2)
    f_right = right[:rim].reshape(2, rows_here + 4, 2)
    t_left = left[rim:].reshape(6, rows_here)
    t_right = right[rim:].reshape(6, rows_here)
    ext = jnp.concatenate([f_left, ext_rows, f_right], axis=2)

    sides = jnp.concatenate([t_left, t_right], axis=1)
    sides = jnp.pad(sides, ((0, 0), (0, cols_here - 2 * rows_here)))
    halo = jnp.stack([t_above, t_below, sides, jnp.zeros_like(sides)], axis=1)
    halo = jnp.concatenate([halo, halo], axis=1)
    vel_main, vel_up, vel_down, vel_side = velocity(idx, all_src, target_geom, halo)
    vel_left = vel_side[0, :rows_here][:, None]
    vel_right = vel_side[0, rows_here:2 * rows_here][:, None]

    vel_rows = jnp.concatenate([vel_up, vel_main, vel_down], axis=0)
    corner = jnp.zeros((1, 1), jnp.float32)
    vel_l = jnp.concatenate([corner, vel_left, corner], axis=0)
    vel_r = jnp.concatenate([corner, vel_right, corner], axis=0)
    vel = jnp.concatenate([vel_l, vel_rows, vel_r], axis=1)
    rates = tendency(ext, vel)
    row_ids = row * rows_here + jnp.arange(rows_here + 2, dtype=jnp.int32) - 1
    col_ids = column * cols_here + jnp.arange(cols_here + 2, dtype=jnp.int32) - 1
    row_ok = (row_ids >= 0) & (row_ids < rows_here * n_tile)
    col_ok = (col_ids >= 0) & (col_ids < cols_here * n_eval)
    inside = (row_ok[:, None] & col_ok[None, :]).astype(jnp.float32)
    smoothed = smooth(rates * inside[None])
    return (eta + 0.5 * smoothed[0], phi + 0.5 * smoothed[1], vel_main)


def solution(mesh):
    return jax.shard_map(
        body,
        mesh=mesh,
        in_specs=(
            P(None, "tile", "eval"),
            P("tile", "eval"),
            P("tile", "eval"),
            P("tile", None, None, "eval"),
            P(),
            P(),
        ),
        out_specs=(P("tile", "eval"), P("tile", "eval"), P("tile", "eval")),
        check_vma=False,
    )
```

```python
import functools

import jax
import jax.numpy as jnp
from jax import lax
from jax.experimental import pallas as pl
from jax.experimental.pallas import tpu as pltpu
from jax.sharding import PartitionSpec as P

ROUNDS = 4
SC = 32
BLOCK = 128

EPS2 = 0.05


def copy_for_each(x, axis):
    peers = lax.axis_size(axis)
    return lax.all_to_all(jnp.broadcast_to(x[None], (peers, *x.shape)), axis, 0, 0, tiled=True)


def from_peer(received, me, offset, peers):
    peer = me + offset
    ok = (peer >= 0) & (peer < peers)
    chunk = lax.dynamic_index_in_dim(received, jnp.clip(peer, 0, peers - 1), 0, keepdims=False)
    return jnp.where(ok, chunk, jnp.zeros_like(chunk))


def velocity_kernel(idx_ref, src_ref, main_ref, halo_ref, out_main_ref, out_up_ref, out_down_ref, out_side_ref):
    total = idx_ref[idx_ref.shape[0] - 1]
    main = tuple(main_ref[k] for k in range(6))
    halo = tuple(halo_ref[k] for k in range(6))
    upper = lax.broadcasted_iota(jnp.int32, main[0].shape, 0) < main[0].shape[0] // 2

    def load(at):
        return src_ref[at], src_ref[at + SC], src_ref[at + 2 * SC], src_ref[at + 3 * SC]

    def term(targ, src, acc):
        tx, ty, tz, nx, ny, nz = targ
        sx, sy, sz, q = src
        dx = tx - sx
        dy = ty - sy
        dz = tz - sz
        dist2 = dx * dx + dy * dy + dz * dz + EPS2
        numer = nx * dx + ny * dy + nz * dz
        r = lax.rsqrt(dist2)
        return acc + (q * numer) * (r * r * r)

    def block(b, accs):
        acc_m, acc_h = accs
        first = b * BLOCK
        for u in range(0, BLOCK, 2):
            one = load(idx_ref[first + u])
            two = load(idx_ref[first + u + 1])
            acc_m = term(main, one, acc_m)
            acc_m = term(main, two, acc_m)
            both = tuple(jnp.where(upper, x, y) for x, y in zip(one, two))
            acc_h = term(halo, both, acc_h)
        return acc_m, acc_h

    blocks = (total + (BLOCK - 1)) // BLOCK
    zero = jnp.zeros(main[0].shape, jnp.float32)
    acc_m, acc_h = lax.fori_loop(0, blocks, block, (zero, zero))
    half = acc_h.shape[0] // 2
    out_main_ref[...] = acc_m
    acc_h = acc_h[:half] + acc_h[half:]
    out_up_ref[...] = acc_h[0:1]
    out_down_ref[...] = acc_h[1:2]
    out_side_ref[...] = acc_h[2:3]


def live_slots(group_len, slots):
    lengths = group_len.T.reshape(-1)
    ends = jnp.cumsum(lengths)
    at = jnp.arange(slots, dtype=jnp.int32)
    passed = ends[None, :] <= at[:, None]
    segment = jnp.sum(passed.astype(jnp.int32), axis=1)
    before = jnp.sum(jnp.where(passed, lengths[None, :], 0), axis=1)
    total = ends[-1]
    idx = jnp.where(at < total, segment * (4 * SC) + (at - before), slots * 4)
    return jnp.concatenate([idx, total[None]])


def velocity(idx, src, main, halo):
    row = jax.ShapeDtypeStruct((1, halo.shape[2]), jnp.float32)
    return pl.pallas_call(
        velocity_kernel,
        out_shape=(jax.ShapeDtypeStruct(main.shape[1:], jnp.float32), row, row, row),
        in_specs=[
            pl.BlockSpec(memory_space=pltpu.SMEM),
            pl.BlockSpec(memory_space=pltpu.SMEM),
            pl.BlockSpec(memory_space=pltpu.VMEM),
            pl.BlockSpec(memory_space=pltpu.VMEM),
        ],
        out_specs=tuple(pl.BlockSpec(memory_space=pltpu.VMEM) for _ in range(4)),
    )(idx, src, main, halo)


def tendency(ext, vel):
    centre = ext[:, 1:-1, 1:-1]
    grad_x = (ext[:, 2:, 1:-1] - ext[:, :-2, 1:-1]) * 0.5
    grad_y = (ext[:, 1:-1, 2:] - ext[:, 1:-1, :-2]) * 0.5
    slope = 1.0 + grad_x[0] * grad_x[0] + grad_y[0] * grad_y[0]
    eta_rate = vel * slope - (grad_x[1] * grad_x[0] + grad_y[1] * grad_y[0])
    phi_rate = (
        -centre[0]
        - 0.5 * (grad_x[1] * grad_x[1] + grad_y[1] * grad_y[1])
        + 0.5 * vel * vel * slope
    )
    return jnp.stack([eta_rate, phi_rate])


def smooth(rim):
    centre = rim[:, 1:-1, 1:-1]
    return (
        4.0 * centre + rim[:, 2:, 1:-1] + rim[:, :-2, 1:-1] + rim[:, 1:-1, 2:] + rim[:, 1:-1, :-2]
    ) / 8.0


def body(target_geom, eta, phi, sources, group_len, owner):
    rows_here, cols_here = eta.shape
    n_tile, n_eval = lax.axis_size("tile"), lax.axis_size("eval")
    row = lax.axis_index("tile")
    column = lax.axis_index("eval")
    width = sources.shape[-1]
    group_len = group_len[:ROUNDS]
    owner = owner[:ROUNDS]

    fields = jnp.stack([eta, phi])
    own_block = sources[0].reshape(-1)
    top = jnp.concatenate([fields[:, :2].reshape(-1), target_geom[:, 0].reshape(-1)])
    bottom = jnp.concatenate([fields[:, -2:].reshape(-1), target_geom[:, -1].reshape(-1)])
    to_above = (jnp.arange(n_tile, dtype=jnp.int32) == row - 1)[:, None]
    payload = jnp.concatenate([
        jnp.broadcast_to(own_block[None], (n_tile, own_block.shape[0])),
        jnp.where(to_above, top[None], bottom[None]),
    ], axis=1)
    got = lax.all_to_all(payload, "tile", 0, 0, tiled=True)
    n_own = own_block.shape[0]
    src_rows = got[:, :n_own].reshape(n_tile, ROUNDS, n_own // ROUNDS)
    stacked = src_rows[owner, jnp.arange(ROUNDS)]
    rim = 2 * cols_here * 2
    above = from_peer(got[:, n_own:], row, -1, n_tile)
    below = from_peer(got[:, n_own:], row, 1, n_tile)
    f_above = above[:rim].reshape(2, 2, cols_here)
    f_below = below[:rim].reshape(2, 2, cols_here)
    t_above = above[rim:].reshape(6, cols_here)
    t_below = below[rim:].reshape(6, cols_here)
    ext_rows = jnp.concatenate([f_above, fields, f_below], axis=1)

    n_src = ROUNDS * 4 * width
    left_rim = jnp.concatenate([ext_rows[:, :, :2].reshape(-1), target_geom[:, :, 0].reshape(-1)])
    right_rim = jnp.concatenate([ext_rows[:, :, -2:].reshape(-1), target_geom[:, :, -1].reshape(-1)])
    to_left = (jnp.arange(n_eval, dtype=jnp.int32) == column - 1)[:, None]
    payload = jnp.concatenate([
        jnp.broadcast_to(stacked.reshape(-1)[None], (n_eval, n_src)),
        jnp.where(to_left, left_rim[None], right_rim[None]),
    ], axis=1)
    got = lax.all_to_all(payload, "eval", 0, 0, tiled=True)
    all_src = jnp.concatenate([got[:, :n_src].reshape(-1), jnp.zeros((4 * SC,), jnp.float32)])
    idx = live_slots(group_len, n_eval * ROUNDS * width)
    rim = 2 * (rows_here + 4) * 2
    left = from_peer(got[:, n_src:], column, -1, n_eval)
    right = from_peer(got[:, n_src:], column, 1, n_eval)
    f_left = left[:rim].reshape(2, rows_here + 4, 2)
    f_right = right[:rim].reshape(2, rows_here + 4, 2)
    t_left = left[rim:].reshape(6, rows_here)
    t_right = right[rim:].reshape(6, rows_here)
    ext = jnp.concatenate([f_left, ext_rows, f_right], axis=2)

    sides = jnp.concatenate([t_left, t_right], axis=1)
    sides = jnp.pad(sides, ((0, 0), (0, cols_here - 2 * rows_here)))
    halo = jnp.stack([t_above, t_below, sides, jnp.zeros_like(sides)], axis=1)
    halo = jnp.concatenate([halo, halo], axis=1)
    vel_main, vel_up, vel_down, vel_side = velocity(idx, all_src, target_geom, halo)
    vel_left = vel_side[0, :rows_here][:, None]
    vel_right = vel_side[0, rows_here:2 * rows_here][:, None]

    vel_rows = jnp.concatenate([vel_up, vel_main, vel_down], axis=0)
    corner = jnp.zeros((1, 1), jnp.float32)
    vel_l = jnp.concatenate([corner, vel_left, corner], axis=0)
    vel_r = jnp.concatenate([corner, vel_right, corner], axis=0)
    vel = jnp.concatenate([vel_l, vel_rows, vel_r], axis=1)
    rates = tendency(ext, vel)
    row_ids = row * rows_here + jnp.arange(rows_here + 2, dtype=jnp.int32) - 1
    col_ids = column * cols_here + jnp.arange(cols_here + 2, dtype=jnp.int32) - 1
    row_ok = (row_ids >= 0) & (row_ids < rows_here * n_tile)
    col_ok = (col_ids >= 0) & (col_ids < cols_here * n_eval)
    inside = (row_ok[:, None] & col_ok[None, :]).astype(jnp.float32)
    smoothed = smooth(rates * inside[None])
    return (eta + 0.5 * smoothed[0], phi + 0.5 * smoothed[1], vel_main)


def solution(mesh):
    return jax.shard_map(
        body,
        mesh=mesh,
        in_specs=(
            P(None, "tile", "eval"),
            P("tile", "eval"),
            P("tile", "eval"),
            P("tile", None, None, "eval"),
            P(),
            P(),
        ),
        out_specs=(P("tile", "eval"), P("tile", "eval"), P("tile", "eval")),
        check_vma=False,
    )
```

```python
import functools

import jax
import jax.numpy as jnp
from jax import lax
from jax.experimental import pallas as pl
from jax.experimental.pallas import tpu as pltpu
from jax.sharding import PartitionSpec as P

ROUNDS = 4
SC = 32
BLOCK = 256

EPS2 = 0.05


def copy_for_each(x, axis):
    peers = lax.axis_size(axis)
    return lax.all_to_all(jnp.broadcast_to(x[None], (peers, *x.shape)), axis, 0, 0, tiled=True)


def from_peer(received, me, offset, peers):
    peer = me + offset
    ok = (peer >= 0) & (peer < peers)
    chunk = lax.dynamic_index_in_dim(received, jnp.clip(peer, 0, peers - 1), 0, keepdims=False)
    return jnp.where(ok, chunk, jnp.zeros_like(chunk))


def velocity_kernel(idx_ref, src_ref, main_ref, halo_ref, out_main_ref, out_up_ref, out_down_ref, out_side_ref):
    total = idx_ref[idx_ref.shape[0] - 1]
    main = tuple(main_ref[k] for k in range(6))
    halo = tuple(halo_ref[k] for k in range(6))
    upper = lax.broadcasted_iota(jnp.int32, main[0].shape, 0) < main[0].shape[0] // 2

    def load(at):
        return src_ref[at], src_ref[at + SC], src_ref[at + 2 * SC], src_ref[at + 3 * SC]

    def term(targ, src, acc):
        tx, ty, tz, nx, ny, nz = targ
        sx, sy, sz, q = src
        dx = tx - sx
        dy = ty - sy
        dz = tz - sz
        dist2 = dx * dx + dy * dy + dz * dz + EPS2
        numer = nx * dx + ny * dy + nz * dz
        r = lax.rsqrt(dist2)
        return acc + (q * numer) * (r * r * r)

    def block(b, accs):
        acc_m, acc_h = accs
        first = b * BLOCK
        for u in range(0, BLOCK, 2):
            one = load(idx_ref[first + u])
            two = load(idx_ref[first + u + 1])
            acc_m = term(main, one, acc_m)
            acc_m = term(main, two, acc_m)
            both = tuple(jnp.where(upper, x, y) for x, y in zip(one, two))
            acc_h = term(halo, both, acc_h)
        return acc_m, acc_h

    blocks = (total + (BLOCK - 1)) // BLOCK
    zero = jnp.zeros(main[0].shape, jnp.float32)
    acc_m, acc_h = lax.fori_loop(0, blocks, block, (zero, zero))
    half = acc_h.shape[0] // 2
    out_main_ref[...] = acc_m
    acc_h = acc_h[:half] + acc_h[half:]
    out_up_ref[...] = acc_h[0:1]
    out_down_ref[...] = acc_h[1:2]
    out_side_ref[...] = acc_h[2:3]


def live_slots(group_len, slots):
    lengths = group_len.T.reshape(-1)
    ends = jnp.cumsum(lengths)
    at = jnp.arange(slots, dtype=jnp.int32)
    passed = ends[None, :] <= at[:, None]
    segment = jnp.sum(passed.astype(jnp.int32), axis=1)
    before = jnp.sum(jnp.where(passed, lengths[None, :], 0), axis=1)
    total = ends[-1]
    idx = jnp.where(at < total, segment * (4 * SC) + (at - before), slots * 4)
    return jnp.concatenate([idx, total[None]])


def velocity(idx, src, main, halo):
    row = jax.ShapeDtypeStruct((1, halo.shape[2]), jnp.float32)
    return pl.pallas_call(
        velocity_kernel,
        out_shape=(jax.ShapeDtypeStruct(main.shape[1:], jnp.float32), row, row, row),
        in_specs=[
            pl.BlockSpec(memory_space=pltpu.SMEM),
            pl.BlockSpec(memory_space=pltpu.SMEM),
            pl.BlockSpec(memory_space=pltpu.VMEM),
            pl.BlockSpec(memory_space=pltpu.VMEM),
        ],
        out_specs=tuple(pl.BlockSpec(memory_space=pltpu.VMEM) for _ in range(4)),
    )(idx, src, main, halo)


def tendency(ext, vel):
    centre = ext[:, 1:-1, 1:-1]
    grad_x = (ext[:, 2:, 1:-1] - ext[:, :-2, 1:-1]) * 0.5
    grad_y = (ext[:, 1:-1, 2:] - ext[:, 1:-1, :-2]) * 0.5
    slope = 1.0 + grad_x[0] * grad_x[0] + grad_y[0] * grad_y[0]
    eta_rate = vel * slope - (grad_x[1] * grad_x[0] + grad_y[1] * grad_y[0])
    phi_rate = (
        -centre[0]
        - 0.5 * (grad_x[1] * grad_x[1] + grad_y[1] * grad_y[1])
        + 0.5 * vel * vel * slope
    )
    return jnp.stack([eta_rate, phi_rate])


def smooth(rim):
    centre = rim[:, 1:-1, 1:-1]
    return (
        4.0 * centre + rim[:, 2:, 1:-1] + rim[:, :-2, 1:-1] + rim[:, 1:-1, 2:] + rim[:, 1:-1, :-2]
    ) / 8.0


def body(target_geom, eta, phi, sources, group_len, owner):
    rows_here, cols_here = eta.shape
    n_tile, n_eval = lax.axis_size("tile"), lax.axis_size("eval")
    row = lax.axis_index("tile")
    column = lax.axis_index("eval")
    width = sources.shape[-1]
    group_len = group_len[:ROUNDS]
    owner = owner[:ROUNDS]

    fields = jnp.stack([eta, phi])
    own_block = sources[0].reshape(-1)
    top = jnp.concatenate([fields[:, :2].reshape(-1), target_geom[:, 0].reshape(-1)])
    bottom = jnp.concatenate([fields[:, -2:].reshape(-1), target_geom[:, -1].reshape(-1)])
    to_above = (jnp.arange(n_tile, dtype=jnp.int32) == row - 1)[:, None]
    payload = jnp.concatenate([
        jnp.broadcast_to(own_block[None], (n_tile, own_block.shape[0])),
        jnp.where(to_above, top[None], bottom[None]),
    ], axis=1)
    got = lax.all_to_all(payload, "tile", 0, 0, tiled=True)
    n_own = own_block.shape[0]
    src_rows = got[:, :n_own].reshape(n_tile, ROUNDS, n_own // ROUNDS)
    stacked = src_rows[owner, jnp.arange(ROUNDS)]
    rim = 2 * cols_here * 2
    above = from_peer(got[:, n_own:], row, -1, n_tile)
    below = from_peer(got[:, n_own:], row, 1, n_tile)
    f_above = above[:rim].reshape(2, 2, cols_here)
    f_below = below[:rim].reshape(2, 2, cols_here)
    t_above = above[rim:].reshape(6, cols_here)
    t_below = below[rim:].reshape(6, cols_here)
    ext_rows = jnp.concatenate([f_above, fields, f_below], axis=1)

    n_src = ROUNDS * 4 * width
    left_rim = jnp.concatenate([ext_rows[:, :, :2].reshape(-1), target_geom[:, :, 0].reshape(-1)])
    right_rim = jnp.concatenate([ext_rows[:, :, -2:].reshape(-1), target_geom[:, :, -1].reshape(-1)])
    to_left = (jnp.arange(n_eval, dtype=jnp.int32) == column - 1)[:, None]
    payload = jnp.concatenate([
        jnp.broadcast_to(stacked.reshape(-1)[None], (n_eval, n_src)),
        jnp.where(to_left, left_rim[None], right_rim[None]),
    ], axis=1)
    got = lax.all_to_all(payload, "eval", 0, 0, tiled=True)
    all_src = jnp.concatenate([got[:, :n_src].reshape(-1), jnp.zeros((4 * SC,), jnp.float32)])
    idx = live_slots(group_len, n_eval * ROUNDS * width)
    rim = 2 * (rows_here + 4) * 2
    left = from_peer(got[:, n_src:], column, -1, n_eval)
    right = from_peer(got[:, n_src:], column, 1, n_eval)
    f_left = left[:rim].reshape(2, rows_here + 4, 2)
    f_right = right[:rim].reshape(2, rows_here + 4, 2)
    t_left = left[rim:].reshape(6, rows_here)
    t_right = right[rim:].reshape(6, rows_here)
    ext = jnp.concatenate([f_left, ext_rows, f_right], axis=2)

    sides = jnp.concatenate([t_left, t_right], axis=1)
    sides = jnp.pad(sides, ((0, 0), (0, cols_here - 2 * rows_here)))
    halo = jnp.stack([t_above, t_below, sides, jnp.zeros_like(sides)], axis=1)
    halo = jnp.concatenate([halo, halo], axis=1)
    vel_main, vel_up, vel_down, vel_side = velocity(idx, all_src, target_geom, halo)
    vel_left = vel_side[0, :rows_here][:, None]
    vel_right = vel_side[0, rows_here:2 * rows_here][:, None]

    vel_rows = jnp.concatenate([vel_up, vel_main, vel_down], axis=0)
    corner = jnp.zeros((1, 1), jnp.float32)
    vel_l = jnp.concatenate([corner, vel_left, corner], axis=0)
    vel_r = jnp.concatenate([corner, vel_right, corner], axis=0)
    vel = jnp.concatenate([vel_l, vel_rows, vel_r], axis=1)
    rates = tendency(ext, vel)
    row_ids = row * rows_here + jnp.arange(rows_here + 2, dtype=jnp.int32) - 1
    col_ids = column * cols_here + jnp.arange(cols_here + 2, dtype=jnp.int32) - 1
    row_ok = (row_ids >= 0) & (row_ids < rows_here * n_tile)
    col_ok = (col_ids >= 0) & (col_ids < cols_here * n_eval)
    inside = (row_ok[:, None] & col_ok[None, :]).astype(jnp.float32)
    smoothed = smooth(rates * inside[None])
    return (eta + 0.5 * smoothed[0], phi + 0.5 * smoothed[1], vel_main)


def solution(mesh):
    return jax.shard_map(
        body,
        mesh=mesh,
        in_specs=(
            P(None, "tile", "eval"),
            P("tile", "eval"),
            P("tile", "eval"),
            P("tile", None, None, "eval"),
            P(),
            P(),
        ),
        out_specs=(P("tile", "eval"), P("tile", "eval"), P("tile", "eval")),
        check_vma=False,
    )
```
